128 devices in a mesh: lat: 8 (over y_lo, z), lon: 16 (over x, y_hi, core).
Axes of the slice: x: 4, y: 4 (y_hi: 2, y_lo: 2; y = y_hi * 2 + y_lo), z: 4, core: 2. Of those that a mesh axis runs over, the one named last changes fastest.
Arguments:
- starting_sea_elevation: float32 [256, 2048], P('lat', 'lon'), may hold values from -6 to 6
- zonal_integrated_flux: float32 [256, 2048], P('lat', 'lon'), may hold values from -6 to 6
- meridional_integrated_flux: float32 [256, 2048], P('lat', 'lon'), may hold values from -6 to 6
- ocean_strata_total: int32 [256, 2048], P('lat', 'lon'), may hold values from 0 to 8
- thermal_anomaly: float32 [8, 256, 2048], P(None, 'lat', 'lon'), may hold values from -6 to 6
- zonal_baroclinic_velocity: float32 [8, 256, 2048], P(None, 'lat', 'lon'), may hold values from -3 to 3
- meridional_baroclinic_velocity: float32 [8, 256, 2048], P(None, 'lat', 'lon'), may hold values from -3 to 3
- sent_sender_mesh_index: int32 [128, 128, 1024], P(('lat', 'lon')), may hold values from 0 to 4095
- sent_intersection_extent: float32 [128, 128, 1024], P(('lat', 'lon')), may hold values from 0.2 to 1
- sent_entry_tally: int32 [128, 128], P(('lat', 'lon')), may hold values from 0 to 1024, as said below
- received_atmosphere_mesh_index: int32 [128, 128, 1024], P(('lat', 'lon')), may hold values from 0 to 4095
Outputs:
- height_new: float32 [256, 2048], P('lat', 'lon')
- east_new: float32 [256, 2048], P('lat', 'lon')
- north_new: float32 [256, 2048], P('lat', 'lon')
- temperature_new: float32 [8, 256, 2048], P(None, 'lat', 'lon')
- atmosphere_fields: float32 [4, 524288], P(None, ('lat', 'lon'))
The draws below stay inside these ranges and needn't reach their ends.
Inputs may be any that keep to these rules, and one draw needn't show every extreme that they name: Slots j >= sent_entry_tally[s, d] are unused. In every draw one owner receives exactly 1024 live slots from every device. `sent_sender_mesh_index`: A cell of the sending device's block, numbered row by row. `received_atmosphere_mesh_index`: an atmosphere cell of the receiving owner. `ocean_strata_total`: 0 is land.
All inputs are finite; a program needn't handle non-finite values.
Results may differ from the reference program's by a relative error of at most 0.00017.
Values sent between devices are 32-bit elements; how exact they have to be, the bound alone decides.
No kernel may reach another device: no remote copies, remote signals or barrier semaphores. Data moves between devices by JAX's collectives and lax.ppermute only.
A program may use at most 64 MiB of HBM per device.

```python
import math
import jax
import jax.numpy as jnp
from jax import lax

CY = 32
CX = 128
VERTICAL_STRATA = 8
STEPS = 4
NF = 4
CAP = 1024
ACELL = 4096
MESH_LATITUDES = 256
MESH_LONGITUDES = 2048
N_LON = 16
DEVICES = 128


def draw_sent_entry_tally(key, part):
    key_one = jax.random.fold_in(key, 11)
    key_two = jax.random.fold_in(key, 12)
    key_full = jax.random.fold_in(key, 13)
    first = jax.random.randint(key_one, (DEVICES, DEVICES), 0, CAP + 1)
    second = jax.random.randint(key_two, (DEVICES, DEVICES), 0, CAP + 1)
    counts = jnp.minimum(first, second)
    full_owner = jax.random.randint(key_full, (), 0, DEVICES)
    column = jnp.arange(DEVICES) == full_owner
    return jnp.where(column[None, :], CAP, counts).astype(jnp.int32)


def with_ends(result, own_key, low, largest):
    dims = result.shape
    spot = [jax.random.randint(jax.random.fold_in(own_key, axis), (), 0, dims[axis]) for axis in range(len(dims))]
    result = result.at[tuple(spot)].set(low)
    longest = dims.index(max(dims))
    spot[longest] = (spot[longest] + 1) % dims[longest]
    return result.at[tuple(spot)].set(largest)


def steps_of(rng, dims, cuts, smallest, largest):
    factor_of, own = 1.0, jax.random.fold_in(rng, 6)
    for axis_at, blocks in cuts:
        steps = jnp.exp(jax.random.uniform(jax.random.fold_in(own, axis_at), (blocks,), jnp.float32, smallest / len(cuts), largest / len(cuts)))
        factor_of = factor_of * jnp.repeat(steps, dims[axis_at] // blocks).reshape([-1 if axis == axis_at else 1 for axis in range(len(dims))])
    return factor_of


def gaussian(rng, shape, spread, reach, shards=(), dtype=jnp.bfloat16):
    drawn = jax.random.normal(rng, shape, jnp.float32) * spread
    if len(shards) > 0:
        drawn = steps_of(rng, shape, shards, -0.22, 0.18) * drawn
    return jnp.clip(drawn, min=-reach, max=reach).astype(dtype)


def setup_inputs(seed: int = 0) -> dict:
    splits = jax.random.split(jax.random.key(seed), 12)
    starting_sea_elevation = gaussian(splits[0], (MESH_LATITUDES, MESH_LONGITUDES), 1.0, 6.0, ((0, 8), (1, 16)), jnp.float32)
    zonal_integrated_flux = gaussian(splits[1], (MESH_LATITUDES, MESH_LONGITUDES), 1.0, 6.0, ((0, 8), (1, 16)), jnp.float32)
    meridional_integrated_flux = gaussian(splits[2], (MESH_LATITUDES, MESH_LONGITUDES), 1.0, 6.0, ((0, 8), (1, 16)), jnp.float32)
    ocean_strata_total = with_ends(jax.random.randint(splits[3], (MESH_LATITUDES, MESH_LONGITUDES), 0, VERTICAL_STRATA + 1), jax.random.fold_in(splits[3], 1), 0, VERTICAL_STRATA).astype(jnp.int32)
    thermal_anomaly = gaussian(splits[4], (VERTICAL_STRATA, MESH_LATITUDES, MESH_LONGITUDES), 1.0, 6.0, ((1, 8), (2, 16)), jnp.float32)
    zonal_baroclinic_velocity = gaussian(splits[5], (VERTICAL_STRATA, MESH_LATITUDES, MESH_LONGITUDES), 0.5, 3.0, ((1, 8), (2, 16)), jnp.float32)
    meridional_baroclinic_velocity = gaussian(splits[6], (VERTICAL_STRATA, MESH_LATITUDES, MESH_LONGITUDES), 0.5, 3.0, ((1, 8), (2, 16)), jnp.float32)
    sent_sender_mesh_index = with_ends(jax.random.randint(splits[7], (DEVICES, DEVICES, CAP), 0, CY * CX), jax.random.fold_in(splits[7], 1), 0, (CY * CX) - 1).astype(jnp.int32)
    sent_intersection_extent = jnp.clip(jnp.exp(math.log(1.0) - 1.609438 * jax.random.uniform(splits[8], (DEVICES, DEVICES, CAP), jnp.float32) ** steps_of(splits[8], (DEVICES, DEVICES, CAP), ((0, 128),), -0.2, 0.2)), 0.2, 1.0)
    sent_entry_tally = draw_sent_entry_tally(jax.random.fold_in(splits[11], 71), 0)
    received_atmosphere_mesh_index = with_ends(jax.random.randint(splits[10], (DEVICES, DEVICES, CAP), 0, ACELL), jax.random.fold_in(splits[10], 1), 0, ACELL - 1).astype(jnp.int32)
    return dict(starting_sea_elevation=starting_sea_elevation, zonal_integrated_flux=zonal_integrated_flux, meridional_integrated_flux=meridional_integrated_flux, ocean_strata_total=ocean_strata_total, thermal_anomaly=thermal_anomaly, zonal_baroclinic_velocity=zonal_baroclinic_velocity, meridional_baroclinic_velocity=meridional_baroclinic_velocity, sent_sender_mesh_index=sent_sender_mesh_index, sent_intersection_extent=sent_intersection_extent, sent_entry_tally=sent_entry_tally, received_atmosphere_mesh_index=received_atmosphere_mesh_index)


mass_coef = 0.7
slope_coef = 0.7
spin_coef = 0.3
mix_coef = 0.1
carry_coef = 0.1


def neighbours(field, sign):
    east = jnp.roll(field, -1, axis=-1)
    west = jnp.roll(field, 1, axis=-1)
    ghost = sign * field[..., -1:, ::-1]
    north = jnp.concatenate([field[..., 1:, :], ghost], axis=-2)
    south = jnp.concatenate([jnp.zeros_like(field[..., :1, :]), field[..., :-1, :]], axis=-2)
    return east, west, north, south


def reference(starting_sea_elevation, zonal_integrated_flux, meridional_integrated_flux, ocean_strata_total, thermal_anomaly, zonal_baroclinic_velocity, meridional_baroclinic_velocity, sent_sender_mesh_index, sent_intersection_extent, sent_entry_tally, received_atmosphere_mesh_index):
    depth = ocean_strata_total.astype(jnp.float32)
    wet = (ocean_strata_total > 0).astype(jnp.float32)
    hnorm = depth / VERTICAL_STRATA
    rows = jnp.arange(MESH_LATITUDES).astype(jnp.float32)
    rotation = (-spin_coef * jnp.cos(jnp.pi * (rows + 0.5) / MESH_LATITUDES))[:, None]
    height = starting_sea_elevation * wet
    east = zonal_integrated_flux * wet
    north = meridional_integrated_flux * wet
    for step in range(STEPS):
        east_e, east_w, _, _ = neighbours(east, -1.0)
        _, _, north_n, north_s = neighbours(north, -1.0)
        height = wet * (height - mass_coef * ((east_e - east_w) + (north_n - north_s)))
        height_e, height_w, height_n, height_s = neighbours(height, 1.0)
        east = wet * (east - slope_coef * hnorm * (height_e - height_w) + rotation * north)
        north = wet * (north - slope_coef * hnorm * (height_n - height_s) - rotation * east)
    levels = jnp.arange(VERTICAL_STRATA).astype(jnp.int32)[:, None, None]
    submerged_stratum_mask = (levels < ocean_strata_total[None]).astype(jnp.float32)
    passive_scalar_values = thermal_anomaly * submerged_stratum_mask
    tracer_e, tracer_w, tracer_n, tracer_s = neighbours(passive_scalar_values, 1.0)
    wet_e, wet_w, wet_n, wet_s = neighbours(submerged_stratum_mask, 1.0)
    mixing = wet_e * (tracer_e - passive_scalar_values) + wet_w * (tracer_w - passive_scalar_values) + wet_n * (tracer_n - passive_scalar_values) + wet_s * (tracer_s - passive_scalar_values)
    speed_east = east[None] + zonal_baroclinic_velocity
    speed_north = north[None] + meridional_baroclinic_velocity
    carried = speed_east * (tracer_e - tracer_w) + speed_north * (tracer_n - tracer_s)
    tracer_new = submerged_stratum_mask * (passive_scalar_values + mix_coef * mixing - carry_coef * carried)
    surface = jnp.stack([height, speed_east[0], speed_north[0], tracer_new[0]]).reshape(NF, -1)
    source = jnp.arange(DEVICES).astype(jnp.int32)[:, None, None]
    grid_row = (source // N_LON) * CY + sent_sender_mesh_index // CX
    grid_col = (source % N_LON) * CX + sent_sender_mesh_index % CX
    flat_index = grid_row * MESH_LONGITUDES + grid_col
    live = jnp.arange(CAP).astype(jnp.int32)[None, None, :] < sent_entry_tally[:, :, None]
    owner = jnp.arange(DEVICES).astype(jnp.int32)[:, None, None]
    target = (owner * ACELL + received_atmosphere_mesh_index).reshape(-1)

    def one_field(field):
        values = jnp.where(live, sent_intersection_extent * field[flat_index], 0.0)
        values = jnp.transpose(values, (1, 0, 2)).reshape(-1)
        return jnp.zeros((DEVICES * ACELL,), jnp.float32).at[target].add(values)

    atmosphere = lax.map(one_field, surface)
    return height, east, north, tracer_new, atmosphere
```

```python
import math

import jax
import jax.numpy as jnp
from jax import lax
from jax.sharding import PartitionSpec as P

VERTICAL_STRATA = 8
STEPS = 4
NF = 4
ACELL = 4096


mass_coef = 0.7
slope_coef = 0.7
spin_coef = 0.3
mix_coef = 0.1
carry_coef = 0.1
block_limit = 8192


HALO = 2 * STEPS


def exchange(block, signs, width):
    planes, rows, columns = block.shape
    sectors = lax.axis_size("lon")
    bands = lax.axis_size("lat")
    eastward = [(i, (i + 1) % sectors) for i in range(sectors)]
    westward = [((i + 1) % sectors, i) for i in range(sectors)]
    from_west = lax.ppermute(block[:, :, columns - width :], "lon", eastward)
    from_east = lax.ppermute(block[:, :, :width], "lon", westward)
    wide = jnp.concatenate([from_west, block, from_east], axis=2)
    upward = [(b, b + 1) for b in range(bands - 1)]
    downward = [(b + 1, b) for b in range(bands - 1)]
    top = wide[:, rows - width :, :]
    from_south = lax.ppermute(top, "lat", upward)
    from_north = lax.ppermute(wide[:, :width, :], "lat", downward)
    last = (bands - 1) * sectors
    mirror = [(last + j, last + sectors - 1 - j) for j in range(sectors)]
    folded = lax.ppermute(top, ("lat", "lon"), mirror)
    folded = jnp.flip(folded, axis=(1, 2)) * signs[:, None, None]
    on_top = lax.axis_index("lat") == bands - 1
    north_rim = jnp.where(on_top, folded, from_north)
    return jnp.concatenate([from_south, wide, north_rim], axis=1)


def east_of(x):
    return jnp.concatenate([x[..., 1:], x[..., -1:]], axis=-1)


def west_of(x):
    return jnp.concatenate([x[..., :1], x[..., :-1]], axis=-1)


def north_of(x):
    return jnp.concatenate([x[..., 1:, :], x[..., -1:, :]], axis=-2)


def south_of(x):
    return jnp.concatenate([x[..., :1, :], x[..., :-1, :]], axis=-2)


def pick_cells(surface_grid, indices):
    fields_count, rows, columns = surface_grid.shape
    table = jnp.transpose(surface_grid, (2, 0, 1)).reshape(columns, fields_count * rows)
    total = indices.shape[0]
    size = math.gcd(total, block_limit)
    blocks = indices.reshape(total // size, size)
    column_ids = jnp.arange(columns)
    row_ids = jnp.arange(rows)

    def one_block(block):
        column_hot = (block[:, None] % columns == column_ids[None, :]).astype(jnp.float32)
        row_hot = (block[:, None] // columns == row_ids[None, :]).astype(jnp.float32)
        by_column = jnp.dot(
            column_hot, table, precision=lax.Precision.HIGHEST, preferred_element_type=jnp.float32
        )
        by_column = by_column.reshape(size, fields_count, rows)
        return jnp.sum(by_column * row_hot[:, None, :], axis=2)

    picked = lax.map(one_block, blocks).reshape(total, fields_count)
    return jnp.transpose(picked)


def spread_cells(values, targets, cells):
    fields_count = values.shape[0]
    total = targets.shape[0]
    size = math.gcd(total, block_limit)
    high_count = cells // 128
    value_blocks = jnp.transpose(values.reshape(fields_count, total // size, size), (1, 0, 2))
    target_blocks = targets.reshape(total // size, size)
    low_ids = jnp.arange(128)
    high_ids = jnp.arange(high_count)

    def add_block(carry, pieces):
        value_block, target_block = pieces
        low_hot = (target_block[:, None] % 128 == low_ids[None, :]).astype(jnp.float32)
        high_hot = (target_block[:, None] // 128 == high_ids[None, :]).astype(jnp.float32)
        weighted = (jnp.transpose(value_block)[:, :, None] * high_hot[:, None, :]).reshape(
            size, fields_count * high_count
        )
        term = lax.dot_general(
            weighted,
            low_hot,
            (((0,), (0,)), ((), ())),
            precision=lax.Precision.HIGHEST,
            preferred_element_type=jnp.float32,
        )
        return (carry + term, None)

    start = jnp.zeros((fields_count * high_count, 128), jnp.float32)
    summed, _ = lax.scan(add_block, start, (value_blocks, target_blocks))
    return summed.reshape(fields_count, cells)


def local(
    starting_sea_elevation,
    zonal_integrated_flux,
    meridional_integrated_flux,
    ocean_strata_total,
    thermal_anomaly,
    zonal_baroclinic_velocity,
    meridional_baroclinic_velocity,
    sent_sender_mesh_index,
    sent_intersection_extent,
    sent_entry_tally,
    received_atmosphere_mesh_index,
):
    band_rows, band_columns = starting_sea_elevation.shape
    grid_rows = band_rows * lax.axis_size("lat")
    band = lax.axis_index("lat")
    depth = ocean_strata_total.astype(jnp.float32)
    planes = jnp.concatenate(
        [
            jnp.stack([starting_sea_elevation, zonal_integrated_flux, meridional_integrated_flux, depth]),
            thermal_anomaly,
        ],
        axis=0,
    )
    signs = jnp.array([1.0, -1.0, -1.0] + [1.0] * (1 + VERTICAL_STRATA), jnp.float32)
    ext = exchange(planes, signs, HALO)
    depth_ext = ext[3]
    wet = (depth_ext > 0).astype(jnp.float32)
    hnorm = depth_ext / VERTICAL_STRATA
    height = ext[0] * wet
    east = ext[1] * wet
    north = ext[2] * wet
    global_rows = band * band_rows - HALO + jnp.arange(band_rows + 2 * HALO)
    global_rows = jnp.where(global_rows >= grid_rows, 2 * grid_rows - 1 - global_rows, global_rows)
    rows = global_rows.astype(jnp.float32)
    rotation = (-spin_coef * jnp.cos(jnp.pi * (rows + 0.5) / grid_rows))[:, None]
    for step in range(STEPS):
        height = wet * (height - mass_coef * (east_of(east) - west_of(east) + (north_of(north) - south_of(north))))
        east = wet * (east - slope_coef * hnorm * (east_of(height) - west_of(height)) + rotation * north)
        north = wet * (north - slope_coef * hnorm * (north_of(height) - south_of(height)) - rotation * east)
    inner = (slice(HALO, HALO + band_rows), slice(HALO, HALO + band_columns))
    height = height[inner]
    east = east[inner]
    north = north[inner]
    near = (slice(None), slice(HALO - 1, HALO + band_rows + 1), slice(HALO - 1, HALO + band_columns + 1))
    levels_float = jnp.arange(VERTICAL_STRATA).astype(jnp.float32)[:, None, None]
    wet_wide = (levels_float < depth_ext[None][near]).astype(jnp.float32)
    tracer_wide = ext[4:][near] * wet_wide
    centre = (slice(None), slice(1, -1), slice(1, -1))
    submerged_stratum_mask = wet_wide[centre]
    passive_scalar_values = tracer_wide[centre]
    tracer_e = east_of(tracer_wide)[centre]
    tracer_w = west_of(tracer_wide)[centre]
    tracer_n = north_of(tracer_wide)[centre]
    tracer_s = south_of(tracer_wide)[centre]
    wet_e = east_of(wet_wide)[centre]
    wet_w = west_of(wet_wide)[centre]
    wet_n = north_of(wet_wide)[centre]
    wet_s = south_of(wet_wide)[centre]
    mixing = (
        wet_e * (tracer_e - passive_scalar_values)
        + wet_w * (tracer_w - passive_scalar_values)
        + wet_n * (tracer_n - passive_scalar_values)
        + wet_s * (tracer_s - passive_scalar_values)
    )
    speed_east = east[None] + zonal_baroclinic_velocity
    speed_north = north[None] + meridional_baroclinic_velocity
    carried = speed_east * (tracer_e - tracer_w) + speed_north * (tracer_n - tracer_s)
    tracer_new = submerged_stratum_mask * (
        passive_scalar_values + mix_coef * mixing - carry_coef * carried
    )
    surface_grid = jnp.stack([height, speed_east[0], speed_north[0], tracer_new[0]])
    owners = sent_sender_mesh_index.shape[1]
    slots = sent_sender_mesh_index.shape[2]
    picked = pick_cells(surface_grid, sent_sender_mesh_index[0].reshape(-1)).reshape(
        NF, owners, slots
    )
    live = jnp.arange(slots)[None, :] < sent_entry_tally[0][:, None]
    values = jnp.where(live[None], sent_intersection_extent[0][None] * picked, 0.0)
    targets = received_atmosphere_mesh_index[0].reshape(-1)
    block = lax.all_to_all(values, ("lat", "lon"), split_axis=1, concat_axis=1, tiled=True)
    fields_count = block.shape[0]
    atmosphere = spread_cells(block.reshape(fields_count, -1), targets, ACELL)
    return (height, east, north, tracer_new, atmosphere)


def solution(mesh):
    in_specs = (
        P("lat", "lon"),
        P("lat", "lon"),
        P("lat", "lon"),
        P("lat", "lon"),
        P(None, "lat", "lon"),
        P(None, "lat", "lon"),
        P(None, "lat", "lon"),
        P(("lat", "lon"), None, None),
        P(("lat", "lon"), None, None),
        P(("lat", "lon"), None),
        P(("lat", "lon"), None, None),
    )
    out_specs = (
        P("lat", "lon"),
        P("lat", "lon"),
        P("lat", "lon"),
        P(None, "lat", "lon"),
        P(None, ("lat", "lon")),
    )
    return jax.shard_map(local, mesh=mesh, in_specs=in_specs, out_specs=out_specs, check_vma=False)
```

```python
import math

import jax
import jax.numpy as jnp
from jax import lax
from jax.experimental import pallas as pl
from jax.sharding import PartitionSpec as P

VERTICAL_STRATA = 8
STEPS = 4
NF = 4
ACELL = 4096


mass_coef = 0.7
slope_coef = 0.7
spin_coef = 0.3
mix_coef = 0.1
carry_coef = 0.1


HALO = 2 * STEPS


def exchange(block, signs, width):
    planes, rows, columns = block.shape
    sectors = lax.axis_size("lon")
    bands = lax.axis_size("lat")
    eastward = [(i, (i + 1) % sectors) for i in range(sectors)]
    westward = [((i + 1) % sectors, i) for i in range(sectors)]
    from_west = lax.ppermute(block[:, :, columns - width :], "lon", eastward)
    from_east = lax.ppermute(block[:, :, :width], "lon", westward)
    wide = jnp.concatenate([from_west, block, from_east], axis=2)
    upward = [(b, b + 1) for b in range(bands - 1)]
    downward = [(b + 1, b) for b in range(bands - 1)]
    top = wide[:, rows - width :, :]
    from_south = lax.ppermute(top, "lat", upward)
    from_north = lax.ppermute(wide[:, :width, :], "lat", downward)
    last = (bands - 1) * sectors
    mirror = [(last + j, last + sectors - 1 - j) for j in range(sectors)]
    folded = lax.ppermute(top, ("lat", "lon"), mirror)
    folded = jnp.flip(folded, axis=(1, 2)) * signs[:, None, None]
    on_top = lax.axis_index("lat") == bands - 1
    north_rim = jnp.where(on_top, folded, from_north)
    return jnp.concatenate([from_south, wide, north_rim], axis=1)


def east_of(x):
    return jnp.concatenate([x[..., 1:], x[..., -1:]], axis=-1)


def west_of(x):
    return jnp.concatenate([x[..., :1], x[..., :-1]], axis=-1)


def north_of(x):
    return jnp.concatenate([x[..., 1:, :], x[..., -1:, :]], axis=-2)


def south_of(x):
    return jnp.concatenate([x[..., :1, :], x[..., :-1, :]], axis=-2)


GROUP = 8


def split_pieces(x):
    high = x.astype(jnp.bfloat16)
    low = (x - high.astype(jnp.float32)).astype(jnp.bfloat16)
    return high, low


def pick_kernel(table_ref, index_ref, extent_ref, tally_ref, out_ref):
    fields_count = out_ref.shape[0]
    slots = index_ref.shape[1]
    table_rows = table_ref.shape[0]
    columns = table_ref.shape[1]
    rows = table_rows // fields_count
    table = jnp.concatenate(split_pieces(table_ref[...]), axis=1)
    column_ids = lax.broadcasted_iota(jnp.int32, (columns, slots), 0)
    row_ids = lax.broadcasted_iota(jnp.int32, (rows, slots), 0)
    slot_ids = lax.broadcasted_iota(jnp.int32, (1, slots), 1)
    for owner in range(index_ref.shape[0]):
        index = index_ref[pl.ds(owner, 1), :]
        hot = (column_ids == index % columns).astype(jnp.bfloat16)
        by_column = jnp.dot(
            table, jnp.concatenate([hot, hot], axis=0), preferred_element_type=jnp.float32
        )
        row_hot = row_ids == index // columns
        weight = jnp.where(
            slot_ids < tally_ref[pl.ds(owner, 1), :], extent_ref[pl.ds(owner, 1), :], 0.0
        )
        for field in range(fields_count):
            part = by_column[field * rows : (field + 1) * rows]
            picked = jnp.sum(jnp.where(row_hot, part, 0.0), axis=0, keepdims=True)
            out_ref[field, pl.ds(owner, 1), :] = picked * weight


def pick_cells(surface_grid, indices, extent, tally):
    fields_count, rows, columns = surface_grid.shape
    owners, slots = indices.shape
    table = surface_grid.reshape(fields_count * rows, columns)
    return pl.pallas_call(
        pick_kernel,
        out_shape=jax.ShapeDtypeStruct((fields_count, owners, slots), jnp.float32),
        grid=(owners // GROUP,),
        in_specs=[
            pl.BlockSpec((fields_count * rows, columns), lambda i: (0, 0)),
            pl.BlockSpec((GROUP, slots), lambda i: (i, 0)),
            pl.BlockSpec((GROUP, slots), lambda i: (i, 0)),
            pl.BlockSpec((GROUP, 1), lambda i: (i, 0)),
        ],
        out_specs=pl.BlockSpec((fields_count, GROUP, slots), lambda i: (0, i, 0)),
    )(table, indices, extent, tally[:, None])


def spread_kernel(value_ref, target_ref, out_ref):
    fields_count = value_ref.shape[0]
    slots = value_ref.shape[2]
    lows = out_ref.shape[1]
    highs = out_ref.shape[0] // fields_count

    @pl.when(pl.program_id(0) == 0)
    def _():
        out_ref[...] = jnp.zeros_like(out_ref)

    high_ids = lax.broadcasted_iota(jnp.int32, (highs, slots), 0)
    low_ids = lax.broadcasted_iota(jnp.int32, (lows, slots), 0)
    total = jnp.zeros(out_ref.shape, jnp.float32)
    for sender in range(target_ref.shape[0]):
        target = target_ref[pl.ds(sender, 1), :]
        high_hot = high_ids == target // lows
        low_hot = (low_ids == target % lows).astype(jnp.bfloat16)
        weighted = jnp.concatenate(
            [
                jnp.where(high_hot, value_ref[field, pl.ds(sender, 1), :], 0.0)
                for field in range(fields_count)
            ],
            axis=0,
        )
        for piece in split_pieces(weighted):
            total = total + lax.dot_general(
                piece, low_hot, (((1,), (1,)), ((), ())), preferred_element_type=jnp.float32
            )
    out_ref[...] += total


def spread_cells(values, targets, cells):
    fields_count, senders, slots = values.shape
    lows = 256
    highs = cells // lows
    summed = pl.pallas_call(
        spread_kernel,
        out_shape=jax.ShapeDtypeStruct((fields_count * highs, lows), jnp.float32),
        grid=(senders // GROUP,),
        in_specs=[
            pl.BlockSpec((fields_count, GROUP, slots), lambda i: (0, i, 0)),
            pl.BlockSpec((GROUP, slots), lambda i: (i, 0)),
        ],
        out_specs=pl.BlockSpec((fields_count * highs, lows), lambda i: (0, 0)),
    )(values, targets)
    return summed.reshape(fields_count, cells)


def local(
    starting_sea_elevation,
    zonal_integrated_flux,
    meridional_integrated_flux,
    ocean_strata_total,
    thermal_anomaly,
    zonal_baroclinic_velocity,
    meridional_baroclinic_velocity,
    sent_sender_mesh_index,
    sent_intersection_extent,
    sent_entry_tally,
    received_atmosphere_mesh_index,
):
    band_rows, band_columns = starting_sea_elevation.shape
    grid_rows = band_rows * lax.axis_size("lat")
    band = lax.axis_index("lat")
    depth = ocean_strata_total.astype(jnp.float32)
    planes = jnp.concatenate(
        [
            jnp.stack([starting_sea_elevation, zonal_integrated_flux, meridional_integrated_flux, depth]),
            thermal_anomaly,
        ],
        axis=0,
    )
    signs = jnp.array([1.0, -1.0, -1.0] + [1.0] * (1 + VERTICAL_STRATA), jnp.float32)
    ext = exchange(planes, signs, HALO)
    depth_ext = ext[3]
    wet = (depth_ext > 0).astype(jnp.float32)
    hnorm = depth_ext / VERTICAL_STRATA
    height = ext[0] * wet
    east = ext[1] * wet
    north = ext[2] * wet
    global_rows = band * band_rows - HALO + jnp.arange(band_rows + 2 * HALO)
    global_rows = jnp.where(global_rows >= grid_rows, 2 * grid_rows - 1 - global_rows, global_rows)
    rows = global_rows.astype(jnp.float32)
    rotation = (-spin_coef * jnp.cos(jnp.pi * (rows + 0.5) / grid_rows))[:, None]
    for step in range(STEPS):
        height = wet * (height - mass_coef * (east_of(east) - west_of(east) + (north_of(north) - south_of(north))))
        east = wet * (east - slope_coef * hnorm * (east_of(height) - west_of(height)) + rotation * north)
        north = wet * (north - slope_coef * hnorm * (north_of(height) - south_of(height)) - rotation * east)
    inner = (slice(HALO, HALO + band_rows), slice(HALO, HALO + band_columns))
    height = height[inner]
    east = east[inner]
    north = north[inner]
    near = (slice(None), slice(HALO - 1, HALO + band_rows + 1), slice(HALO - 1, HALO + band_columns + 1))
    levels_float = jnp.arange(VERTICAL_STRATA).astype(jnp.float32)[:, None, None]
    wet_wide = (levels_float < depth_ext[None][near]).astype(jnp.float32)
    tracer_wide = ext[4:][near] * wet_wide
    centre = (slice(None), slice(1, -1), slice(1, -1))
    submerged_stratum_mask = wet_wide[centre]
    passive_scalar_values = tracer_wide[centre]
    tracer_e = east_of(tracer_wide)[centre]
    tracer_w = west_of(tracer_wide)[centre]
    tracer_n = north_of(tracer_wide)[centre]
    tracer_s = south_of(tracer_wide)[centre]
    wet_e = east_of(wet_wide)[centre]
    wet_w = west_of(wet_wide)[centre]
    wet_n = north_of(wet_wide)[centre]
    wet_s = south_of(wet_wide)[centre]
    mixing = (
        wet_e * (tracer_e - passive_scalar_values)
        + wet_w * (tracer_w - passive_scalar_values)
        + wet_n * (tracer_n - passive_scalar_values)
        + wet_s * (tracer_s - passive_scalar_values)
    )
    speed_east = east[None] + zonal_baroclinic_velocity
    speed_north = north[None] + meridional_baroclinic_velocity
    carried = speed_east * (tracer_e - tracer_w) + speed_north * (tracer_n - tracer_s)
    tracer_new = submerged_stratum_mask * (
        passive_scalar_values + mix_coef * mixing - carry_coef * carried
    )
    surface_grid = jnp.stack([height, speed_east[0], speed_north[0], tracer_new[0]])
    values = pick_cells(
        surface_grid, sent_sender_mesh_index[0], sent_intersection_extent[0], sent_entry_tally[0]
    )
    block = lax.all_to_all(values, ("lat", "lon"), split_axis=1, concat_axis=1, tiled=True)
    atmosphere = spread_cells(block, received_atmosphere_mesh_index[0], ACELL)
    return (height, east, north, tracer_new, atmosphere)


def solution(mesh):
    in_specs = (
        P("lat", "lon"),
        P("lat", "lon"),
        P("lat", "lon"),
        P("lat", "lon"),
        P(None, "lat", "lon"),
        P(None, "lat", "lon"),
        P(None, "lat", "lon"),
        P(("lat", "lon"), None, None),
        P(("lat", "lon"), None, None),
        P(("lat", "lon"), None),
        P(("lat", "lon"), None, None),
    )
    out_specs = (
        P("lat", "lon"),
        P("lat", "lon"),
        P("lat", "lon"),
        P(None, "lat", "lon"),
        P(None, ("lat", "lon")),
    )
    return jax.shard_map(local, mesh=mesh, in_specs=in_specs, out_specs=out_specs, check_vma=False)
```

```python
import math

import jax
import jax.numpy as jnp
from jax import lax
from jax.experimental import pallas as pl
from jax.sharding import PartitionSpec as P

VERTICAL_STRATA = 8
STEPS = 4
NF = 4
ACELL = 4096


mass_coef = 0.7
slope_coef = 0.7
spin_coef = 0.3
mix_coef = 0.1
carry_coef = 0.1


HALO = 2 * STEPS


def exchange(block, signs, width):
    planes, rows, columns = block.shape
    sectors = lax.axis_size("lon")
    bands = lax.axis_size("lat")
    eastward = [(i, (i + 1) % sectors) for i in range(sectors)]
    westward = [((i + 1) % sectors, i) for i in range(sectors)]
    from_west = lax.ppermute(block[:, :, columns - width :], "lon", eastward)
    from_east = lax.ppermute(block[:, :, :width], "lon", westward)
    wide = jnp.concatenate([from_west, block, from_east], axis=2)
    upward = [(b, b + 1) for b in range(bands - 1)]
    downward = [(b + 1, b) for b in range(bands - 1)]
    top = wide[:, rows - width :, :]
    from_south = lax.ppermute(top, "lat", upward)
    from_north = lax.ppermute(wide[:, :width, :], "lat", downward)
    last = (bands - 1) * sectors
    mirror = [(last + j, last + sectors - 1 - j) for j in range(sectors)]
    folded = lax.ppermute(top, ("lat", "lon"), mirror)
    folded = jnp.flip(folded, axis=(1, 2)) * signs[:, None, None]
    on_top = lax.axis_index("lat") == bands - 1
    north_rim = jnp.where(on_top, folded, from_north)
    return jnp.concatenate([from_south, wide, north_rim], axis=1)


def east_of(x):
    return jnp.concatenate([x[..., 1:], x[..., -1:]], axis=-1)


def west_of(x):
    return jnp.concatenate([x[..., :1], x[..., :-1]], axis=-1)


def north_of(x):
    return jnp.concatenate([x[..., 1:, :], x[..., -1:, :]], axis=-2)


def south_of(x):
    return jnp.concatenate([x[..., :1, :], x[..., :-1, :]], axis=-2)


GROUP = 8


def split_pieces(x):
    high = x.astype(jnp.bfloat16)
    low = (x - high.astype(jnp.float32)).astype(jnp.bfloat16)
    return high, low


def pick_kernel(table_ref, index_ref, extent_ref, tally_ref, out_ref):
    fields_count = out_ref.shape[0]
    slots = index_ref.shape[1]
    table_rows = table_ref.shape[0]
    columns = table_ref.shape[1]
    rows = table_rows // fields_count
    table = jnp.concatenate(split_pieces(table_ref[...]), axis=1)
    column_ids = lax.broadcasted_iota(jnp.int32, (columns, slots), 0)
    row_ids = lax.broadcasted_iota(jnp.int32, (8, slots), 0)
    slot_ids = lax.broadcasted_iota(jnp.int32, (1, slots), 1)
    for owner in range(index_ref.shape[0]):
        index = index_ref[pl.ds(owner, 1), :]
        hot = (column_ids == index % columns).astype(jnp.bfloat16)
        by_column = jnp.dot(
            table, jnp.concatenate([hot, hot], axis=0), preferred_element_type=jnp.float32
        )
        row = index // columns
        masks = [row_ids + 8 * tile == row for tile in range(rows // 8)]
        weight = jnp.where(
            slot_ids < tally_ref[pl.ds(owner, 1), :], extent_ref[pl.ds(owner, 1), :], 0.0
        )
        for field in range(fields_count):
            chosen = jnp.zeros((8, slots), jnp.float32)
            for tile in range(rows // 8):
                start = field * rows + tile * 8
                chosen = jnp.where(masks[tile], by_column[start : start + 8], chosen)
            picked = jnp.sum(chosen, axis=0, keepdims=True)
            out_ref[field, pl.ds(owner, 1), :] = picked * weight


def pick_cells(surface_grid, indices, extent, tally):
    fields_count, rows, columns = surface_grid.shape
    owners, slots = indices.shape
    table = surface_grid.reshape(fields_count * rows, columns)
    return pl.pallas_call(
        pick_kernel,
        out_shape=jax.ShapeDtypeStruct((fields_count, owners, slots), jnp.float32),
        grid=(owners // GROUP,),
        in_specs=[
            pl.BlockSpec((fields_count * rows, columns), lambda i: (0, 0)),
            pl.BlockSpec((GROUP, slots), lambda i: (i, 0)),
            pl.BlockSpec((GROUP, slots), lambda i: (i, 0)),
            pl.BlockSpec((GROUP, 1), lambda i: (i, 0)),
        ],
        out_specs=pl.BlockSpec((fields_count, GROUP, slots), lambda i: (0, i, 0)),
    )(table, indices, extent, tally[:, None])


def spread_kernel(value_ref, target_ref, out_ref):
    fields_count = value_ref.shape[0]
    slots = value_ref.shape[2]
    lows = out_ref.shape[0]
    highs = out_ref.shape[1] // (2 * fields_count)

    @pl.when(pl.program_id(0) == 0)
    def _():
        out_ref[...] = jnp.zeros_like(out_ref)

    high_ids = lax.broadcasted_iota(jnp.int32, (highs, slots), 0)
    low_ids = lax.broadcasted_iota(jnp.int32, (lows, slots), 0)
    total = jnp.zeros(out_ref.shape, jnp.float32)
    for sender in range(target_ref.shape[0]):
        target = target_ref[pl.ds(sender, 1), :]
        high_hot = high_ids == target // lows
        low_hot = (low_ids == target % lows).astype(jnp.bfloat16)
        pieces = []
        for field in range(fields_count):
            high, low_part = split_pieces(value_ref[field, pl.ds(sender, 1), :])
            pieces.append((high, low_part))
        weighted = jnp.concatenate(
            [
                jnp.where(high_hot, pieces[field][part].astype(jnp.float32), 0.0).astype(jnp.bfloat16)
                for part in range(2)
                for field in range(fields_count)
            ],
            axis=0,
        )
        total = total + lax.dot_general(
            low_hot, weighted, (((1,), (1,)), ((), ())), preferred_element_type=jnp.float32
        )
    out_ref[...] += total


def spread_cells(values, targets, cells):
    fields_count, senders, slots = values.shape
    lows = 128
    highs = cells // lows
    summed = pl.pallas_call(
        spread_kernel,
        out_shape=jax.ShapeDtypeStruct((lows, 2 * fields_count * highs), jnp.float32),
        grid=(senders // GROUP,),
        in_specs=[
            pl.BlockSpec((fields_count, GROUP, slots), lambda i: (0, i, 0)),
            pl.BlockSpec((GROUP, slots), lambda i: (i, 0)),
        ],
        out_specs=pl.BlockSpec((lows, 2 * fields_count * highs), lambda i: (0, 0)),
    )(values, targets)
    summed = summed.reshape(lows, 2, fields_count, highs).sum(axis=1)
    return jnp.transpose(summed, (1, 2, 0)).reshape(fields_count, cells)


def local(
    starting_sea_elevation,
    zonal_integrated_flux,
    meridional_integrated_flux,
    ocean_strata_total,
    thermal_anomaly,
    zonal_baroclinic_velocity,
    meridional_baroclinic_velocity,
    sent_sender_mesh_index,
    sent_intersection_extent,
    sent_entry_tally,
    received_atmosphere_mesh_index,
):
    band_rows, band_columns = starting_sea_elevation.shape
    grid_rows = band_rows * lax.axis_size("lat")
    band = lax.axis_index("lat")
    depth = ocean_strata_total.astype(jnp.float32)
    planes = jnp.concatenate(
        [
            jnp.stack([starting_sea_elevation, zonal_integrated_flux, meridional_integrated_flux, depth]),
            thermal_anomaly,
        ],
        axis=0,
    )
    signs = jnp.array([1.0, -1.0, -1.0] + [1.0] * (1 + VERTICAL_STRATA), jnp.float32)
    ext = exchange(planes, signs, HALO)
    depth_ext = ext[3]
    wet = (depth_ext > 0).astype(jnp.float32)
    hnorm = depth_ext / VERTICAL_STRATA
    height = ext[0] * wet
    east = ext[1] * wet
    north = ext[2] * wet
    global_rows = band * band_rows - HALO + jnp.arange(band_rows + 2 * HALO)
    global_rows = jnp.where(global_rows >= grid_rows, 2 * grid_rows - 1 - global_rows, global_rows)
    rows = global_rows.astype(jnp.float32)
    rotation = (-spin_coef * jnp.cos(jnp.pi * (rows + 0.5) / grid_rows))[:, None]
    for step in range(STEPS):
        height = wet * (height - mass_coef * (east_of(east) - west_of(east) + (north_of(north) - south_of(north))))
        east = wet * (east - slope_coef * hnorm * (east_of(height) - west_of(height)) + rotation * north)
        north = wet * (north - slope_coef * hnorm * (north_of(height) - south_of(height)) - rotation * east)
    inner = (slice(HALO, HALO + band_rows), slice(HALO, HALO + band_columns))
    height = height[inner]
    east = east[inner]
    north = north[inner]
    near = (slice(None), slice(HALO - 1, HALO + band_rows + 1), slice(HALO - 1, HALO + band_columns + 1))
    levels_float = jnp.arange(VERTICAL_STRATA).astype(jnp.float32)[:, None, None]
    wet_wide = (levels_float < depth_ext[None][near]).astype(jnp.float32)
    tracer_wide = ext[4:][near] * wet_wide
    centre = (slice(None), slice(1, -1), slice(1, -1))
    submerged_stratum_mask = wet_wide[centre]
    passive_scalar_values = tracer_wide[centre]
    tracer_e = east_of(tracer_wide)[centre]
    tracer_w = west_of(tracer_wide)[centre]
    tracer_n = north_of(tracer_wide)[centre]
    tracer_s = south_of(tracer_wide)[centre]
    wet_e = east_of(wet_wide)[centre]
    wet_w = west_of(wet_wide)[centre]
    wet_n = north_of(wet_wide)[centre]
    wet_s = south_of(wet_wide)[centre]
    mixing = (
        wet_e * (tracer_e - passive_scalar_values)
        + wet_w * (tracer_w - passive_scalar_values)
        + wet_n * (tracer_n - passive_scalar_values)
        + wet_s * (tracer_s - passive_scalar_values)
    )
    speed_east = east[None] + zonal_baroclinic_velocity
    speed_north = north[None] + meridional_baroclinic_velocity
    carried = speed_east * (tracer_e - tracer_w) + speed_north * (tracer_n - tracer_s)
    tracer_new = submerged_stratum_mask * (
        passive_scalar_values + mix_coef * mixing - carry_coef * carried
    )
    surface_grid = jnp.stack([height, speed_east[0], speed_north[0], tracer_new[0]])
    values = pick_cells(
        surface_grid, sent_sender_mesh_index[0], sent_intersection_extent[0], sent_entry_tally[0]
    )
    block = lax.all_to_all(values, ("lat", "lon"), split_axis=1, concat_axis=1, tiled=True)
    atmosphere = spread_cells(block, received_atmosphere_mesh_index[0], ACELL)
    return (height, east, north, tracer_new, atmosphere)


def solution(mesh):
    in_specs = (
        P("lat", "lon"),
        P("lat", "lon"),
        P("lat", "lon"),
        P("lat", "lon"),
        P(None, "lat", "lon"),
        P(None, "lat", "lon"),
        P(None, "lat", "lon"),
        P(("lat", "lon"), None, None),
        P(("lat", "lon"), None, None),
        P(("lat", "lon"), None),
        P(("lat", "lon"), None, None),
    )
    out_specs = (
        P("lat", "lon"),
        P("lat", "lon"),
        P("lat", "lon"),
        P(None, "lat", "lon"),
        P(None, ("lat", "lon")),
    )
    return jax.shard_map(local, mesh=mesh, in_specs=in_specs, out_specs=out_specs, check_vma=False)
```

```python
import math

import jax
import jax.numpy as jnp
from jax import lax
from jax.experimental import pallas as pl
from jax.sharding import PartitionSpec as P

VERTICAL_STRATA = 8
STEPS = 4
NF = 4
ACELL = 4096


mass_coef = 0.7
slope_coef = 0.7
spin_coef = 0.3
mix_coef = 0.1
carry_coef = 0.1


HALO = 2 * STEPS


def exchange(block, signs, width):
    planes, rows, columns = block.shape
    sectors = lax.axis_size("lon")
    bands = lax.axis_size("lat")
    eastward = [(i, (i + 1) % sectors) for i in range(sectors)]
    westward = [((i + 1) % sectors, i) for i in range(sectors)]
    from_west = lax.ppermute(block[:, :, columns - width :], "lon", eastward)
    from_east = lax.ppermute(block[:, :, :width], "lon", westward)
    wide = jnp.concatenate([from_west, block, from_east], axis=2)
    upward = [(b, b + 1) for b in range(bands - 1)]
    downward = [(b + 1, b) for b in range(bands - 1)]
    top = wide[:, rows - width :, :]
    from_south = lax.ppermute(top, "lat", upward)
    from_north = lax.ppermute(wide[:, :width, :], "lat", downward)
    last = (bands - 1) * sectors
    mirror = [(last + j, last + sectors - 1 - j) for j in range(sectors)]
    folded = lax.ppermute(top, ("lat", "lon"), mirror)
    folded = jnp.flip(folded, axis=(1, 2)) * signs[:, None, None]
    on_top = lax.axis_index("lat") == bands - 1
    north_rim = jnp.where(on_top, folded, from_north)
    return jnp.concatenate([from_south, wide, north_rim], axis=1)


def east_of(x):
    return jnp.concatenate([x[..., 1:], x[..., -1:]], axis=-1)


def west_of(x):
    return jnp.concatenate([x[..., :1], x[..., :-1]], axis=-1)


def north_of(x):
    return jnp.concatenate([x[..., 1:, :], x[..., -1:, :]], axis=-2)


def south_of(x):
    return jnp.concatenate([x[..., :1, :], x[..., :-1, :]], axis=-2)


GROUP = 8


def split_pieces(x):
    high = x.astype(jnp.bfloat16)
    low = (x - high.astype(jnp.float32)).astype(jnp.bfloat16)
    return high, low


def pick_kernel(table_ref, index_ref, extent_ref, tally_ref, out_ref):
    fields_count = out_ref.shape[1]
    slots = index_ref.shape[1]
    table_rows = table_ref.shape[0]
    columns = table_ref.shape[1]
    rows = table_rows // fields_count
    table = jnp.concatenate(split_pieces(table_ref[...]), axis=1)
    column_ids = lax.broadcasted_iota(jnp.int32, (columns, slots), 0)
    row_ids = lax.broadcasted_iota(jnp.int32, (8, slots), 0)
    slot_ids = lax.broadcasted_iota(jnp.int32, (1, slots), 1)
    for owner in range(index_ref.shape[0]):
        index = index_ref[pl.ds(owner, 1), :]
        hot = (column_ids == index % columns).astype(jnp.bfloat16)
        by_column = jnp.dot(
            table, jnp.concatenate([hot, hot], axis=0), preferred_element_type=jnp.float32
        )
        row = index // columns
        masks = [row_ids + 8 * tile == row for tile in range(rows // 8)]
        weight = jnp.where(
            slot_ids < tally_ref[pl.ds(owner, 1), :], extent_ref[pl.ds(owner, 1), :], 0.0
        )
        for field in range(fields_count):
            chosen = jnp.zeros((8, slots), jnp.float32)
            for tile in range(rows // 8):
                start = field * rows + tile * 8
                chosen = jnp.where(masks[tile], by_column[start : start + 8], chosen)
            picked = jnp.sum(chosen, axis=0, keepdims=True)
            out_ref[owner, pl.ds(field, 1), :] = picked * weight


def pick_cells(surface_grid, indices, extent, tally):
    fields_count, rows, columns = surface_grid.shape
    owners, slots = indices.shape
    table = surface_grid.reshape(fields_count * rows, columns)
    return pl.pallas_call(
        pick_kernel,
        out_shape=jax.ShapeDtypeStruct((owners, fields_count, slots), jnp.float32),
        grid=(owners // GROUP,),
        in_specs=[
            pl.BlockSpec((fields_count * rows, columns), lambda i: (0, 0)),
            pl.BlockSpec((GROUP, slots), lambda i: (i, 0)),
            pl.BlockSpec((GROUP, slots), lambda i: (i, 0)),
            pl.BlockSpec((GROUP, 1), lambda i: (i, 0)),
        ],
        out_specs=pl.BlockSpec((GROUP, fields_count, slots), lambda i: (i, 0, 0)),
    )(table, indices, extent, tally[:, None])


def spread_kernel(value_ref, target_ref, out_ref):
    fields_count = value_ref.shape[1]
    slots = value_ref.shape[2]
    lows = out_ref.shape[0]
    highs = out_ref.shape[1] // (2 * fields_count)

    @pl.when(pl.program_id(0) == 0)
    def _():
        out_ref[...] = jnp.zeros_like(out_ref)

    high_ids = lax.broadcasted_iota(jnp.int32, (highs, slots), 0)
    low_ids = lax.broadcasted_iota(jnp.int32, (lows, slots), 0)
    total = jnp.zeros(out_ref.shape, jnp.float32)
    for sender in range(target_ref.shape[0]):
        target = target_ref[pl.ds(sender, 1), :]
        high_hot = high_ids == target // lows
        low_hot = (low_ids == target % lows).astype(jnp.bfloat16)
        pieces = []
        for field in range(fields_count):
            high, low_part = split_pieces(value_ref[sender, pl.ds(field, 1), :])
            pieces.append((high, low_part))
        weighted = jnp.concatenate(
            [
                jnp.where(high_hot, pieces[field][part].astype(jnp.float32), 0.0).astype(jnp.bfloat16)
                for part in range(2)
                for field in range(fields_count)
            ],
            axis=0,
        )
        total = total + lax.dot_general(
            low_hot, weighted, (((1,), (1,)), ((), ())), preferred_element_type=jnp.float32
        )
    out_ref[...] += total


def spread_cells(values, targets, cells):
    senders, fields_count, slots = values.shape
    lows = 128
    highs = cells // lows
    summed = pl.pallas_call(
        spread_kernel,
        out_shape=jax.ShapeDtypeStruct((lows, 2 * fields_count * highs), jnp.float32),
        grid=(senders // GROUP,),
        in_specs=[
            pl.BlockSpec((GROUP, fields_count, slots), lambda i: (i, 0, 0)),
            pl.BlockSpec((GROUP, slots), lambda i: (i, 0)),
        ],
        out_specs=pl.BlockSpec((lows, 2 * fields_count * highs), lambda i: (0, 0)),
    )(values, targets)
    summed = summed.reshape(lows, 2, fields_count, highs).sum(axis=1)
    return jnp.transpose(summed, (1, 2, 0)).reshape(fields_count, cells)


def local(
    starting_sea_elevation,
    zonal_integrated_flux,
    meridional_integrated_flux,
    ocean_strata_total,
    thermal_anomaly,
    zonal_baroclinic_velocity,
    meridional_baroclinic_velocity,
    sent_sender_mesh_index,
    sent_intersection_extent,
    sent_entry_tally,
    received_atmosphere_mesh_index,
):
    band_rows, band_columns = starting_sea_elevation.shape
    grid_rows = band_rows * lax.axis_size("lat")
    band = lax.axis_index("lat")
    depth = ocean_strata_total.astype(jnp.float32)
    planes = jnp.concatenate(
        [
            jnp.stack([starting_sea_elevation, zonal_integrated_flux, meridional_integrated_flux, depth]),
            thermal_anomaly,
        ],
        axis=0,
    )
    signs = jnp.array([1.0, -1.0, -1.0] + [1.0] * (1 + VERTICAL_STRATA), jnp.float32)
    ext = exchange(planes, signs, HALO)
    depth_ext = ext[3]
    wet = (depth_ext > 0).astype(jnp.float32)
    hnorm = depth_ext / VERTICAL_STRATA
    height = ext[0] * wet
    east = ext[1] * wet
    north = ext[2] * wet
    global_rows = band * band_rows - HALO + jnp.arange(band_rows + 2 * HALO)
    global_rows = jnp.where(global_rows >= grid_rows, 2 * grid_rows - 1 - global_rows, global_rows)
    rows = global_rows.astype(jnp.float32)
    rotation = (-spin_coef * jnp.cos(jnp.pi * (rows + 0.5) / grid_rows))[:, None]
    for step in range(STEPS):
        height = wet * (height - mass_coef * (east_of(east) - west_of(east) + (north_of(north) - south_of(north))))
        east = wet * (east - slope_coef * hnorm * (east_of(height) - west_of(height)) + rotation * north)
        north = wet * (north - slope_coef * hnorm * (north_of(height) - south_of(height)) - rotation * east)
    inner = (slice(HALO, HALO + band_rows), slice(HALO, HALO + band_columns))
    height = height[inner]
    east = east[inner]
    north = north[inner]
    near = (slice(None), slice(HALO - 1, HALO + band_rows + 1), slice(HALO - 1, HALO + band_columns + 1))
    levels_float = jnp.arange(VERTICAL_STRATA).astype(jnp.float32)[:, None, None]
    wet_wide = (levels_float < depth_ext[None][near]).astype(jnp.float32)
    tracer_wide = ext[4:][near] * wet_wide
    centre = (slice(None), slice(1, -1), slice(1, -1))
    submerged_stratum_mask = wet_wide[centre]
    passive_scalar_values = tracer_wide[centre]
    tracer_e = east_of(tracer_wide)[centre]
    tracer_w = west_of(tracer_wide)[centre]
    tracer_n = north_of(tracer_wide)[centre]
    tracer_s = south_of(tracer_wide)[centre]
    wet_e = east_of(wet_wide)[centre]
    wet_w = west_of(wet_wide)[centre]
    wet_n = north_of(wet_wide)[centre]
    wet_s = south_of(wet_wide)[centre]
    mixing = (
        wet_e * (tracer_e - passive_scalar_values)
        + wet_w * (tracer_w - passive_scalar_values)
        + wet_n * (tracer_n - passive_scalar_values)
        + wet_s * (tracer_s - passive_scalar_values)
    )
    speed_east = east[None] + zonal_baroclinic_velocity
    speed_north = north[None] + meridional_baroclinic_velocity
    carried = speed_east * (tracer_e - tracer_w) + speed_north * (tracer_n - tracer_s)
    tracer_new = submerged_stratum_mask * (
        passive_scalar_values + mix_coef * mixing - carry_coef * carried
    )
    surface_grid = jnp.stack([height, speed_east[0], speed_north[0], tracer_new[0]])
    values = pick_cells(
        surface_grid, sent_sender_mesh_index[0], sent_intersection_extent[0], sent_entry_tally[0]
    )
    block = lax.all_to_all(values, ("lat", "lon"), split_axis=0, concat_axis=0, tiled=True)
    atmosphere = spread_cells(block, received_atmosphere_mesh_index[0], ACELL)
    return (height, east, north, tracer_new, atmosphere)


def solution(mesh):
    in_specs = (
        P("lat", "lon"),
        P("lat", "lon"),
        P("lat", "lon"),
        P("lat", "lon"),
        P(None, "lat", "lon"),
        P(None, "lat", "lon"),
        P(None, "lat", "lon"),
        P(("lat", "lon"), None, None),
        P(("lat", "lon"), None, None),
        P(("lat", "lon"), None),
        P(("lat", "lon"), None, None),
    )
    out_specs = (
        P("lat", "lon"),
        P("lat", "lon"),
        P("lat", "lon"),
        P(None, "lat", "lon"),
        P(None, ("lat", "lon")),
    )
    return jax.shard_map(local, mesh=mesh, in_specs=in_specs, out_specs=out_specs, check_vma=False)
```

```python
import math

import jax
import jax.numpy as jnp
from jax import lax
from jax.experimental import pallas as pl
from jax.sharding import PartitionSpec as P

VERTICAL_STRATA = 8
STEPS = 4
NF = 4
ACELL = 4096


mass_coef = 0.7
slope_coef = 0.7
spin_coef = 0.3
mix_coef = 0.1
carry_coef = 0.1


HALO = 2 * STEPS


def exchange(block, signs, width):
    planes, rows, columns = block.shape
    sectors = lax.axis_size("lon")
    bands = lax.axis_size("lat")
    eastward = [(i, (i + 1) % sectors) for i in range(sectors)]
    westward = [((i + 1) % sectors, i) for i in range(sectors)]
    from_west = lax.ppermute(block[:, :, columns - width :], "lon", eastward)
    from_east = lax.ppermute(block[:, :, :width], "lon", westward)
    wide = jnp.concatenate([from_west, block, from_east], axis=2)
    upward = [(b, b + 1) for b in range(bands - 1)]
    downward = [(b + 1, b) for b in range(bands - 1)]
    top = wide[:, rows - width :, :]
    from_south = lax.ppermute(top, "lat", upward)
    from_north = lax.ppermute(wide[:, :width, :], "lat", downward)
    last = (bands - 1) * sectors
    mirror = [(last + j, last + sectors - 1 - j) for j in range(sectors)]
    folded = lax.ppermute(top, ("lat", "lon"), mirror)
    folded = jnp.flip(folded, axis=(1, 2)) * signs[:, None, None]
    on_top = lax.axis_index("lat") == bands - 1
    north_rim = jnp.where(on_top, folded, from_north)
    return jnp.concatenate([from_south, wide, north_rim], axis=1)


def east_of(x):
    return jnp.concatenate([x[..., 1:], x[..., -1:]], axis=-1)


def west_of(x):
    return jnp.concatenate([x[..., :1], x[..., :-1]], axis=-1)


def north_of(x):
    return jnp.concatenate([x[..., 1:, :], x[..., -1:, :]], axis=-2)


def south_of(x):
    return jnp.concatenate([x[..., :1, :], x[..., :-1, :]], axis=-2)


GROUP = 8
CHUNKS = 2


def split_pieces(x):
    high = x.astype(jnp.bfloat16)
    low = (x - high.astype(jnp.float32)).astype(jnp.bfloat16)
    return high, low


def pick_kernel(table_ref, index_ref, extent_ref, tally_ref, out_ref):
    fields_count = out_ref.shape[1]
    slots = index_ref.shape[1]
    table_rows = table_ref.shape[0]
    columns = table_ref.shape[1]
    rows = table_rows // fields_count
    table = jnp.concatenate(split_pieces(table_ref[...]), axis=1)
    column_ids = lax.broadcasted_iota(jnp.int32, (columns, slots), 0)
    row_ids = lax.broadcasted_iota(jnp.int32, (8, slots), 0)
    slot_ids = lax.broadcasted_iota(jnp.int32, (1, slots), 1)
    for owner in range(index_ref.shape[0]):
        index = index_ref[pl.ds(owner, 1), :]
        hot = (column_ids == index % columns).astype(jnp.bfloat16)
        by_column = jnp.dot(
            table, jnp.concatenate([hot, hot], axis=0), preferred_element_type=jnp.float32
        )
        row = index // columns
        masks = [row_ids + 8 * tile == row for tile in range(rows // 8)]
        weight = jnp.where(
            slot_ids < tally_ref[pl.ds(owner, 1), :], extent_ref[pl.ds(owner, 1), :], 0.0
        )
        for field in range(fields_count):
            chosen = jnp.zeros((8, slots), jnp.float32)
            for tile in range(rows // 8):
                start = field * rows + tile * 8
                chosen = jnp.where(masks[tile], by_column[start : start + 8], chosen)
            picked = jnp.sum(chosen, axis=0, keepdims=True)
            out_ref[owner, pl.ds(field, 1), :] = picked * weight


def pick_cells(surface_grid, indices, extent, tally):
    fields_count, rows, columns = surface_grid.shape
    owners, slots = indices.shape
    table = surface_grid.reshape(fields_count * rows, columns)
    return pl.pallas_call(
        pick_kernel,
        out_shape=jax.ShapeDtypeStruct((owners, fields_count, slots), jnp.float32),
        grid=(owners // GROUP,),
        in_specs=[
            pl.BlockSpec((fields_count * rows, columns), lambda i: (0, 0)),
            pl.BlockSpec((GROUP, slots), lambda i: (i, 0)),
            pl.BlockSpec((GROUP, slots), lambda i: (i, 0)),
            pl.BlockSpec((GROUP, 1), lambda i: (i, 0)),
        ],
        out_specs=pl.BlockSpec((GROUP, fields_count, slots), lambda i: (i, 0, 0)),
    )(table, indices, extent, tally[:, None])


def spread_kernel(value_ref, target_ref, out_ref):
    fields_count = value_ref.shape[1]
    slots = value_ref.shape[2]
    lows = out_ref.shape[0]
    highs = out_ref.shape[1] // (2 * fields_count)

    @pl.when(pl.program_id(0) == 0)
    def _():
        out_ref[...] = jnp.zeros_like(out_ref)

    high_ids = lax.broadcasted_iota(jnp.int32, (highs, slots), 0)
    low_ids = lax.broadcasted_iota(jnp.int32, (lows, slots), 0)
    total = jnp.zeros(out_ref.shape, jnp.float32)
    for sender in range(target_ref.shape[0]):
        target = target_ref[pl.ds(sender, 1), :]
        high_hot = high_ids == target // lows
        low_hot = (low_ids == target % lows).astype(jnp.bfloat16)
        pieces = []
        for field in range(fields_count):
            high, low_part = split_pieces(value_ref[sender, pl.ds(field, 1), :])
            pieces.append((high, low_part))
        weighted = jnp.concatenate(
            [
                jnp.where(high_hot, pieces[field][part].astype(jnp.float32), 0.0).astype(jnp.bfloat16)
                for part in range(2)
                for field in range(fields_count)
            ],
            axis=0,
        )
        total = total + lax.dot_general(
            low_hot, weighted, (((1,), (1,)), ((), ())), preferred_element_type=jnp.float32
        )
    out_ref[...] += total


def spread_cells(values, targets, cells):
    senders, fields_count, slots = values.shape
    lows = 128
    highs = cells // lows
    summed = pl.pallas_call(
        spread_kernel,
        out_shape=jax.ShapeDtypeStruct((lows, 2 * fields_count * highs), jnp.float32),
        grid=(senders // GROUP,),
        in_specs=[
            pl.BlockSpec((GROUP, fields_count, slots), lambda i: (i, 0, 0)),
            pl.BlockSpec((GROUP, slots), lambda i: (i, 0)),
        ],
        out_specs=pl.BlockSpec((lows, 2 * fields_count * highs), lambda i: (0, 0)),
    )(values, targets)
    summed = summed.reshape(lows, 2, fields_count, highs).sum(axis=1)
    return jnp.transpose(summed, (1, 2, 0)).reshape(fields_count, cells)


def local(
    starting_sea_elevation,
    zonal_integrated_flux,
    meridional_integrated_flux,
    ocean_strata_total,
    thermal_anomaly,
    zonal_baroclinic_velocity,
    meridional_baroclinic_velocity,
    sent_sender_mesh_index,
    sent_intersection_extent,
    sent_entry_tally,
    received_atmosphere_mesh_index,
):
    band_rows, band_columns = starting_sea_elevation.shape
    grid_rows = band_rows * lax.axis_size("lat")
    band = lax.axis_index("lat")
    depth = ocean_strata_total.astype(jnp.float32)
    planes = jnp.concatenate(
        [
            jnp.stack([starting_sea_elevation, zonal_integrated_flux, meridional_integrated_flux, depth]),
            thermal_anomaly,
        ],
        axis=0,
    )
    signs = jnp.array([1.0, -1.0, -1.0] + [1.0] * (1 + VERTICAL_STRATA), jnp.float32)
    ext = exchange(planes, signs, HALO)
    depth_ext = ext[3]
    wet = (depth_ext > 0).astype(jnp.float32)
    hnorm = depth_ext / VERTICAL_STRATA
    height = ext[0] * wet
    east = ext[1] * wet
    north = ext[2] * wet
    global_rows = band * band_rows - HALO + jnp.arange(band_rows + 2 * HALO)
    global_rows = jnp.where(global_rows >= grid_rows, 2 * grid_rows - 1 - global_rows, global_rows)
    rows = global_rows.astype(jnp.float32)
    rotation = (-spin_coef * jnp.cos(jnp.pi * (rows + 0.5) / grid_rows))[:, None]
    for step in range(STEPS):
        height = wet * (height - mass_coef * (east_of(east) - west_of(east) + (north_of(north) - south_of(north))))
        east = wet * (east - slope_coef * hnorm * (east_of(height) - west_of(height)) + rotation * north)
        north = wet * (north - slope_coef * hnorm * (north_of(height) - south_of(height)) - rotation * east)
    inner = (slice(HALO, HALO + band_rows), slice(HALO, HALO + band_columns))
    height = height[inner]
    east = east[inner]
    north = north[inner]
    near = (slice(None), slice(HALO - 1, HALO + band_rows + 1), slice(HALO - 1, HALO + band_columns + 1))
    levels_float = jnp.arange(VERTICAL_STRATA).astype(jnp.float32)[:, None, None]
    wet_wide = (levels_float < depth_ext[None][near]).astype(jnp.float32)
    tracer_wide = ext[4:][near] * wet_wide
    centre = (slice(None), slice(1, -1), slice(1, -1))
    submerged_stratum_mask = wet_wide[centre]
    passive_scalar_values = tracer_wide[centre]
    tracer_e = east_of(tracer_wide)[centre]
    tracer_w = west_of(tracer_wide)[centre]
    tracer_n = north_of(tracer_wide)[centre]
    tracer_s = south_of(tracer_wide)[centre]
    wet_e = east_of(wet_wide)[centre]
    wet_w = west_of(wet_wide)[centre]
    wet_n = north_of(wet_wide)[centre]
    wet_s = south_of(wet_wide)[centre]
    mixing = (
        wet_e * (tracer_e - passive_scalar_values)
        + wet_w * (tracer_w - passive_scalar_values)
        + wet_n * (tracer_n - passive_scalar_values)
        + wet_s * (tracer_s - passive_scalar_values)
    )
    speed_east = east[None] + zonal_baroclinic_velocity
    speed_north = north[None] + meridional_baroclinic_velocity
    carried = speed_east * (tracer_e - tracer_w) + speed_north * (tracer_n - tracer_s)
    tracer_new = submerged_stratum_mask * (
        passive_scalar_values + mix_coef * mixing - carry_coef * carried
    )
    surface_grid = jnp.stack([height, speed_east[0], speed_north[0], tracer_new[0]])
    slots = sent_sender_mesh_index.shape[2]
    width = slots // CHUNKS
    atmosphere = 0.0
    for chunk in range(CHUNKS):
        part = slice(chunk * width, (chunk + 1) * width)
        values = pick_cells(
            surface_grid,
            sent_sender_mesh_index[0][:, part],
            sent_intersection_extent[0][:, part],
            sent_entry_tally[0] - chunk * width,
        )
        block = lax.all_to_all(values, ("lat", "lon"), split_axis=0, concat_axis=0, tiled=True)
        atmosphere = atmosphere + spread_cells(block, received_atmosphere_mesh_index[0][:, part], ACELL)
    return (height, east, north, tracer_new, atmosphere)


def solution(mesh):
    in_specs = (
        P("lat", "lon"),
        P("lat", "lon"),
        P("lat", "lon"),
        P("lat", "lon"),
        P(None, "lat", "lon"),
        P(None, "lat", "lon"),
        P(None, "lat", "lon"),
        P(("lat", "lon"), None, None),
        P(("lat", "lon"), None, None),
        P(("lat", "lon"), None),
        P(("lat", "lon"), None, None),
    )
    out_specs = (
        P("lat", "lon"),
        P("lat", "lon"),
        P("lat", "lon"),
        P(None, "lat", "lon"),
        P(None, ("lat", "lon")),
    )
    return jax.shard_map(local, mesh=mesh, in_specs=in_specs, out_specs=out_specs, check_vma=False)
```

```python
import math

import jax
import jax.numpy as jnp
from jax import lax
from jax.experimental import pallas as pl
from jax.sharding import PartitionSpec as P

VERTICAL_STRATA = 8
STEPS = 4
NF = 4
ACELL = 4096


mass_coef = 0.7
slope_coef = 0.7
spin_coef = 0.3
mix_coef = 0.1
carry_coef = 0.1


HALO = 2 * STEPS


def exchange(block, signs, width):
    planes, rows, columns = block.shape
    sectors = lax.axis_size("lon")
    bands = lax.axis_size("lat")
    eastward = [(i, (i + 1) % sectors) for i in range(sectors)]
    westward = [((i + 1) % sectors, i) for i in range(sectors)]
    from_west = lax.ppermute(block[:, :, columns - width :], "lon", eastward)
    from_east = lax.ppermute(block[:, :, :width], "lon", westward)
    wide = jnp.concatenate([from_west, block, from_east], axis=2)
    upward = [(b, b + 1) for b in range(bands - 1)]
    downward = [(b + 1, b) for b in range(bands - 1)]
    top = wide[:, rows - width :, :]
    from_south = lax.ppermute(top, "lat", upward)
    from_north = lax.ppermute(wide[:, :width, :], "lat", downward)
    last = (bands - 1) * sectors
    mirror = [(last + j, last + sectors - 1 - j) for j in range(sectors)]
    folded = lax.ppermute(top, ("lat", "lon"), mirror)
    folded = jnp.flip(folded, axis=(1, 2)) * signs[:, None, None]
    on_top = lax.axis_index("lat") == bands - 1
    north_rim = jnp.where(on_top, folded, from_north)
    return jnp.concatenate([from_south, wide, north_rim], axis=1)


def east_of(x):
    return jnp.concatenate([x[..., 1:], x[..., -1:]], axis=-1)


def west_of(x):
    return jnp.concatenate([x[..., :1], x[..., :-1]], axis=-1)


def north_of(x):
    return jnp.concatenate([x[..., 1:, :], x[..., -1:, :]], axis=-2)


def south_of(x):
    return jnp.concatenate([x[..., :1, :], x[..., :-1, :]], axis=-2)


GROUP = 8
CHUNKS = 4


def split_pieces(x):
    high = x.astype(jnp.bfloat16)
    low = (x - high.astype(jnp.float32)).astype(jnp.bfloat16)
    return high, low


def pick_kernel(table_ref, index_ref, extent_ref, tally_ref, out_ref):
    fields_count = out_ref.shape[1]
    slots = index_ref.shape[1]
    table_rows = table_ref.shape[0]
    columns = table_ref.shape[1]
    rows = table_rows // fields_count
    table = jnp.concatenate(split_pieces(table_ref[...]), axis=1)
    column_ids = lax.broadcasted_iota(jnp.int32, (columns, slots), 0)
    row_ids = lax.broadcasted_iota(jnp.int32, (8, slots), 0)
    slot_ids = lax.broadcasted_iota(jnp.int32, (1, slots), 1)
    for owner in range(index_ref.shape[0]):
        index = index_ref[pl.ds(owner, 1), :]
        hot = (column_ids == index % columns).astype(jnp.bfloat16)
        by_column = jnp.dot(
            table, jnp.concatenate([hot, hot], axis=0), preferred_element_type=jnp.float32
        )
        row = index // columns
        masks = [row_ids + 8 * tile == row for tile in range(rows // 8)]
        weight = jnp.where(
            slot_ids < tally_ref[pl.ds(owner, 1), :], extent_ref[pl.ds(owner, 1), :], 0.0
        )
        for field in range(fields_count):
            chosen = jnp.zeros((8, slots), jnp.float32)
            for tile in range(rows // 8):
                start = field * rows + tile * 8
                chosen = jnp.where(masks[tile], by_column[start : start + 8], chosen)
            picked = jnp.sum(chosen, axis=0, keepdims=True)
            out_ref[owner, pl.ds(field, 1), :] = picked * weight


def pick_cells(surface_grid, indices, extent, tally):
    fields_count, rows, columns = surface_grid.shape
    owners, slots = indices.shape
    table = surface_grid.reshape(fields_count * rows, columns)
    return pl.pallas_call(
        pick_kernel,
        out_shape=jax.ShapeDtypeStruct((owners, fields_count, slots), jnp.float32),
        grid=(owners // GROUP,),
        in_specs=[
            pl.BlockSpec((fields_count * rows, columns), lambda i: (0, 0)),
            pl.BlockSpec((GROUP, slots), lambda i: (i, 0)),
            pl.BlockSpec((GROUP, slots), lambda i: (i, 0)),
            pl.BlockSpec((GROUP, 1), lambda i: (i, 0)),
        ],
        out_specs=pl.BlockSpec((GROUP, fields_count, slots), lambda i: (i, 0, 0)),
    )(table, indices, extent, tally[:, None])


def spread_kernel(value_ref, target_ref, out_ref):
    fields_count = value_ref.shape[1]
    slots = value_ref.shape[2]
    lows = out_ref.shape[0]
    highs = out_ref.shape[1] // (2 * fields_count)

    @pl.when(pl.program_id(0) == 0)
    def _():
        out_ref[...] = jnp.zeros_like(out_ref)

    high_ids = lax.broadcasted_iota(jnp.int32, (highs, slots), 0)
    low_ids = lax.broadcasted_iota(jnp.int32, (lows, slots), 0)
    total = jnp.zeros(out_ref.shape, jnp.float32)
    for sender in range(target_ref.shape[0]):
        target = target_ref[pl.ds(sender, 1), :]
        high_hot = high_ids == target // lows
        low_hot = (low_ids == target % lows).astype(jnp.bfloat16)
        pieces = []
        for field in range(fields_count):
            high, low_part = split_pieces(value_ref[sender, pl.ds(field, 1), :])
            pieces.append((high, low_part))
        weighted = jnp.concatenate(
            [
                jnp.where(high_hot, pieces[field][part].astype(jnp.float32), 0.0).astype(jnp.bfloat16)
                for part in range(2)
                for field in range(fields_count)
            ],
            axis=0,
        )
        total = total + lax.dot_general(
            low_hot, weighted, (((1,), (1,)), ((), ())), preferred_element_type=jnp.float32
        )
    out_ref[...] += total


def spread_cells(values, targets, cells):
    senders, fields_count, slots = values.shape
    lows = 128
    highs = cells // lows
    summed = pl.pallas_call(
        spread_kernel,
        out_shape=jax.ShapeDtypeStruct((lows, 2 * fields_count * highs), jnp.float32),
        grid=(senders // GROUP,),
        in_specs=[
            pl.BlockSpec((GROUP, fields_count, slots), lambda i: (i, 0, 0)),
            pl.BlockSpec((GROUP, slots), lambda i: (i, 0)),
        ],
        out_specs=pl.BlockSpec((lows, 2 * fields_count * highs), lambda i: (0, 0)),
    )(values, targets)
    summed = summed.reshape(lows, 2, fields_count, highs).sum(axis=1)
    return jnp.transpose(summed, (1, 2, 0)).reshape(fields_count, cells)


def local(
    starting_sea_elevation,
    zonal_integrated_flux,
    meridional_integrated_flux,
    ocean_strata_total,
    thermal_anomaly,
    zonal_baroclinic_velocity,
    meridional_baroclinic_velocity,
    sent_sender_mesh_index,
    sent_intersection_extent,
    sent_entry_tally,
    received_atmosphere_mesh_index,
):
    band_rows, band_columns = starting_sea_elevation.shape
    grid_rows = band_rows * lax.axis_size("lat")
    band = lax.axis_index("lat")
    depth = ocean_strata_total.astype(jnp.float32)
    planes = jnp.concatenate(
        [
            jnp.stack([starting_sea_elevation, zonal_integrated_flux, meridional_integrated_flux, depth]),
            thermal_anomaly,
        ],
        axis=0,
    )
    signs = jnp.array([1.0, -1.0, -1.0] + [1.0] * (1 + VERTICAL_STRATA), jnp.float32)
    ext = exchange(planes, signs, HALO)
    depth_ext = ext[3]
    wet = (depth_ext > 0).astype(jnp.float32)
    hnorm = depth_ext / VERTICAL_STRATA
    height = ext[0] * wet
    east = ext[1] * wet
    north = ext[2] * wet
    global_rows = band * band_rows - HALO + jnp.arange(band_rows + 2 * HALO)
    global_rows = jnp.where(global_rows >= grid_rows, 2 * grid_rows - 1 - global_rows, global_rows)
    rows = global_rows.astype(jnp.float32)
    rotation = (-spin_coef * jnp.cos(jnp.pi * (rows + 0.5) / grid_rows))[:, None]
    for step in range(STEPS):
        height = wet * (height - mass_coef * (east_of(east) - west_of(east) + (north_of(north) - south_of(north))))
        east = wet * (east - slope_coef * hnorm * (east_of(height) - west_of(height)) + rotation * north)
        north = wet * (north - slope_coef * hnorm * (north_of(height) - south_of(height)) - rotation * east)
    inner = (slice(HALO, HALO + band_rows), slice(HALO, HALO + band_columns))
    height = height[inner]
    east = east[inner]
    north = north[inner]
    near = (slice(None), slice(HALO - 1, HALO + band_rows + 1), slice(HALO - 1, HALO + band_columns + 1))
    levels_float = jnp.arange(VERTICAL_STRATA).astype(jnp.float32)[:, None, None]
    wet_wide = (levels_float < depth_ext[None][near]).astype(jnp.float32)
    tracer_wide = ext[4:][near] * wet_wide
    centre = (slice(None), slice(1, -1), slice(1, -1))
    submerged_stratum_mask = wet_wide[centre]
    passive_scalar_values = tracer_wide[centre]
    tracer_e = east_of(tracer_wide)[centre]
    tracer_w = west_of(tracer_wide)[centre]
    tracer_n = north_of(tracer_wide)[centre]
    tracer_s = south_of(tracer_wide)[centre]
    wet_e = east_of(wet_wide)[centre]
    wet_w = west_of(wet_wide)[centre]
    wet_n = north_of(wet_wide)[centre]
    wet_s = south_of(wet_wide)[centre]
    mixing = (
        wet_e * (tracer_e - passive_scalar_values)
        + wet_w * (tracer_w - passive_scalar_values)
        + wet_n * (tracer_n - passive_scalar_values)
        + wet_s * (tracer_s - passive_scalar_values)
    )
    speed_east = east[None] + zonal_baroclinic_velocity
    speed_north = north[None] + meridional_baroclinic_velocity
    carried = speed_east * (tracer_e - tracer_w) + speed_north * (tracer_n - tracer_s)
    tracer_new = submerged_stratum_mask * (
        passive_scalar_values + mix_coef * mixing - carry_coef * carried
    )
    surface_grid = jnp.stack([height, speed_east[0], speed_north[0], tracer_new[0]])
    slots = sent_sender_mesh_index.shape[2]
    width = slots // CHUNKS
    atmosphere = 0.0
    for chunk in range(CHUNKS):
        part = slice(chunk * width, (chunk + 1) * width)
        values = pick_cells(
            surface_grid,
            sent_sender_mesh_index[0][:, part],
            sent_intersection_extent[0][:, part],
            sent_entry_tally[0] - chunk * width,
        )
        block = lax.all_to_all(values, ("lat", "lon"), split_axis=0, concat_axis=0, tiled=True)
        atmosphere = atmosphere + spread_cells(block, received_atmosphere_mesh_index[0][:, part], ACELL)
    return (height, east, north, tracer_new, atmosphere)


def solution(mesh):
    in_specs = (
        P("lat", "lon"),
        P("lat", "lon"),
        P("lat", "lon"),
        P("lat", "lon"),
        P(None, "lat", "lon"),
        P(None, "lat", "lon"),
        P(None, "lat", "lon"),
        P(("lat", "lon"), None, None),
        P(("lat", "lon"), None, None),
        P(("lat", "lon"), None),
        P(("lat", "lon"), None, None),
    )
    out_specs = (
        P("lat", "lon"),
        P("lat", "lon"),
        P("lat", "lon"),
        P(None, "lat", "lon"),
        P(None, ("lat", "lon")),
    )
    return jax.shard_map(local, mesh=mesh, in_specs=in_specs, out_specs=out_specs, check_vma=False)
```

```python
import math

import jax
import jax.numpy as jnp
from jax import lax
from jax.experimental import pallas as pl
from jax.sharding import PartitionSpec as P

VERTICAL_STRATA = 8
STEPS = 4
NF = 4
ACELL = 4096


mass_coef = 0.7
slope_coef = 0.7
spin_coef = 0.3
mix_coef = 0.1
carry_coef = 0.1


HALO = 2 * STEPS


def exchange(block, signs, width):
    planes, rows, columns = block.shape
    sectors = lax.axis_size("lon")
    bands = lax.axis_size("lat")
    eastward = [(i, (i + 1) % sectors) for i in range(sectors)]
    westward = [((i + 1) % sectors, i) for i in range(sectors)]
    from_west = lax.ppermute(block[:, :, columns - width :], "lon", eastward)
    from_east = lax.ppermute(block[:, :, :width], "lon", westward)
    wide = jnp.concatenate([from_west, block, from_east], axis=2)
    upward = [(b, b + 1) for b in range(bands - 1)]
    downward = [(b + 1, b) for b in range(bands - 1)]
    top = wide[:, rows - width :, :]
    from_south = lax.ppermute(top, "lat", upward)
    from_north = lax.ppermute(wide[:, :width, :], "lat", downward)
    last = (bands - 1) * sectors
    mirror = [(last + j, last + sectors - 1 - j) for j in range(sectors)]
    folded = lax.ppermute(top, ("lat", "lon"), mirror)
    folded = jnp.flip(folded, axis=(1, 2)) * signs[:, None, None]
    on_top = lax.axis_index("lat") == bands - 1
    north_rim = jnp.where(on_top, folded, from_north)
    return jnp.concatenate([from_south, wide, north_rim], axis=1)


def east_of(x):
    return jnp.concatenate([x[..., 1:], x[..., -1:]], axis=-1)


def west_of(x):
    return jnp.concatenate([x[..., :1], x[..., :-1]], axis=-1)


def north_of(x):
    return jnp.concatenate([x[..., 1:, :], x[..., -1:, :]], axis=-2)


def south_of(x):
    return jnp.concatenate([x[..., :1, :], x[..., :-1, :]], axis=-2)


GROUP = 32
CHUNKS = 2


def split_pieces(x):
    high = x.astype(jnp.bfloat16)
    low = (x - high.astype(jnp.float32)).astype(jnp.bfloat16)
    return high, low


def pick_kernel(table_ref, index_ref, extent_ref, tally_ref, out_ref):
    fields_count = out_ref.shape[1]
    slots = index_ref.shape[1]
    table_rows = table_ref.shape[0]
    columns = table_ref.shape[1]
    rows = table_rows // fields_count
    table = jnp.concatenate(split_pieces(table_ref[...]), axis=1)
    column_ids = lax.broadcasted_iota(jnp.int32, (columns, slots), 0)
    row_ids = lax.broadcasted_iota(jnp.int32, (8, slots), 0)
    slot_ids = lax.broadcasted_iota(jnp.int32, (1, slots), 1)
    for owner in range(index_ref.shape[0]):
        index = index_ref[pl.ds(owner, 1), :]
        hot = (column_ids == index % columns).astype(jnp.bfloat16)
        by_column = jnp.dot(
            table, jnp.concatenate([hot, hot], axis=0), preferred_element_type=jnp.float32
        )
        row = index // columns
        masks = [row_ids + 8 * tile == row for tile in range(rows // 8)]
        weight = jnp.where(
            slot_ids < tally_ref[pl.ds(owner, 1), :], extent_ref[pl.ds(owner, 1), :], 0.0
        )
        for field in range(fields_count):
            chosen = jnp.zeros((8, slots), jnp.float32)
            for tile in range(rows // 8):
                start = field * rows + tile * 8
                chosen = jnp.where(masks[tile], by_column[start : start + 8], chosen)
            picked = jnp.sum(chosen, axis=0, keepdims=True)
            out_ref[owner, pl.ds(field, 1), :] = picked * weight


def pick_cells(surface_grid, indices, extent, tally):
    fields_count, rows, columns = surface_grid.shape
    owners, slots = indices.shape
    table = surface_grid.reshape(fields_count * rows, columns)
    return pl.pallas_call(
        pick_kernel,
        out_shape=jax.ShapeDtypeStruct((owners, fields_count, slots), jnp.float32),
        grid=(owners // GROUP,),
        in_specs=[
            pl.BlockSpec((fields_count * rows, columns), lambda i: (0, 0)),
            pl.BlockSpec((GROUP, slots), lambda i: (i, 0)),
            pl.BlockSpec((GROUP, slots), lambda i: (i, 0)),
            pl.BlockSpec((GROUP, 1), lambda i: (i, 0)),
        ],
        out_specs=pl.BlockSpec((GROUP, fields_count, slots), lambda i: (i, 0, 0)),
    )(table, indices, extent, tally[:, None])


def spread_kernel(value_ref, target_ref, out_ref):
    fields_count = value_ref.shape[1]
    slots = value_ref.shape[2]
    lows = out_ref.shape[0]
    highs = out_ref.shape[1] // (2 * fields_count)

    @pl.when(pl.program_id(0) == 0)
    def _():
        out_ref[...] = jnp.zeros_like(out_ref)

    high_ids = lax.broadcasted_iota(jnp.int32, (highs, slots), 0)
    low_ids = lax.broadcasted_iota(jnp.int32, (lows, slots), 0)
    total = jnp.zeros(out_ref.shape, jnp.float32)
    for sender in range(target_ref.shape[0]):
        target = target_ref[pl.ds(sender, 1), :]
        high_hot = high_ids == target // lows
        low_hot = (low_ids == target % lows).astype(jnp.bfloat16)
        pieces = []
        for field in range(fields_count):
            high, low_part = split_pieces(value_ref[sender, pl.ds(field, 1), :])
            pieces.append((high, low_part))
        weighted = jnp.concatenate(
            [
                jnp.where(high_hot, pieces[field][part].astype(jnp.float32), 0.0).astype(jnp.bfloat16)
                for part in range(2)
                for field in range(fields_count)
            ],
            axis=0,
        )
        total = total + lax.dot_general(
            low_hot, weighted, (((1,), (1,)), ((), ())), preferred_element_type=jnp.float32
        )
    out_ref[...] += total


def spread_cells(values, targets, cells):
    senders, fields_count, slots = values.shape
    lows = 128
    highs = cells // lows
    summed = pl.pallas_call(
        spread_kernel,
        out_shape=jax.ShapeDtypeStruct((lows, 2 * fields_count * highs), jnp.float32),
        grid=(senders // GROUP,),
        in_specs=[
            pl.BlockSpec((GROUP, fields_count, slots), lambda i: (i, 0, 0)),
            pl.BlockSpec((GROUP, slots), lambda i: (i, 0)),
        ],
        out_specs=pl.BlockSpec((lows, 2 * fields_count * highs), lambda i: (0, 0)),
    )(values, targets)
    summed = summed.reshape(lows, 2, fields_count, highs).sum(axis=1)
    return jnp.transpose(summed, (1, 2, 0)).reshape(fields_count, cells)


def local(
    starting_sea_elevation,
    zonal_integrated_flux,
    meridional_integrated_flux,
    ocean_strata_total,
    thermal_anomaly,
    zonal_baroclinic_velocity,
    meridional_baroclinic_velocity,
    sent_sender_mesh_index,
    sent_intersection_extent,
    sent_entry_tally,
    received_atmosphere_mesh_index,
):
    band_rows, band_columns = starting_sea_elevation.shape
    grid_rows = band_rows * lax.axis_size("lat")
    band = lax.axis_index("lat")
    depth = ocean_strata_total.astype(jnp.float32)
    planes = jnp.concatenate(
        [
            jnp.stack([starting_sea_elevation, zonal_integrated_flux, meridional_integrated_flux, depth]),
            thermal_anomaly,
        ],
        axis=0,
    )
    signs = jnp.array([1.0, -1.0, -1.0] + [1.0] * (1 + VERTICAL_STRATA), jnp.float32)
    ext = exchange(planes, signs, HALO)
    depth_ext = ext[3]
    wet = (depth_ext > 0).astype(jnp.float32)
    hnorm = depth_ext / VERTICAL_STRATA
    height = ext[0] * wet
    east = ext[1] * wet
    north = ext[2] * wet
    global_rows = band * band_rows - HALO + jnp.arange(band_rows + 2 * HALO)
    global_rows = jnp.where(global_rows >= grid_rows, 2 * grid_rows - 1 - global_rows, global_rows)
    rows = global_rows.astype(jnp.float32)
    rotation = (-spin_coef * jnp.cos(jnp.pi * (rows + 0.5) / grid_rows))[:, None]
    for step in range(STEPS):
        height = wet * (height - mass_coef * (east_of(east) - west_of(east) + (north_of(north) - south_of(north))))
        east = wet * (east - slope_coef * hnorm * (east_of(height) - west_of(height)) + rotation * north)
        north = wet * (north - slope_coef * hnorm * (north_of(height) - south_of(height)) - rotation * east)
    inner = (slice(HALO, HALO + band_rows), slice(HALO, HALO + band_columns))
    height = height[inner]
    east = east[inner]
    north = north[inner]
    near = (slice(None), slice(HALO - 1, HALO + band_rows + 1), slice(HALO - 1, HALO + band_columns + 1))
    levels_float = jnp.arange(VERTICAL_STRATA).astype(jnp.float32)[:, None, None]
    wet_wide = (levels_float < depth_ext[None][near]).astype(jnp.float32)
    tracer_wide = ext[4:][near] * wet_wide
    centre = (slice(None), slice(1, -1), slice(1, -1))
    submerged_stratum_mask = wet_wide[centre]
    passive_scalar_values = tracer_wide[centre]
    tracer_e = east_of(tracer_wide)[centre]
    tracer_w = west_of(tracer_wide)[centre]
    tracer_n = north_of(tracer_wide)[centre]
    tracer_s = south_of(tracer_wide)[centre]
    wet_e = east_of(wet_wide)[centre]
    wet_w = west_of(wet_wide)[centre]
    wet_n = north_of(wet_wide)[centre]
    wet_s = south_of(wet_wide)[centre]
    mixing = (
        wet_e * (tracer_e - passive_scalar_values)
        + wet_w * (tracer_w - passive_scalar_values)
        + wet_n * (tracer_n - passive_scalar_values)
        + wet_s * (tracer_s - passive_scalar_values)
    )
    speed_east = east[None] + zonal_baroclinic_velocity
    speed_north = north[None] + meridional_baroclinic_velocity
    carried = speed_east * (tracer_e - tracer_w) + speed_north * (tracer_n - tracer_s)
    tracer_new = submerged_stratum_mask * (
        passive_scalar_values + mix_coef * mixing - carry_coef * carried
    )
    surface_grid = jnp.stack([height, speed_east[0], speed_north[0], tracer_new[0]])
    slots = sent_sender_mesh_index.shape[2]
    width = slots // CHUNKS
    atmosphere = 0.0
    for chunk in range(CHUNKS):
        part = slice(chunk * width, (chunk + 1) * width)
        values = pick_cells(
            surface_grid,
            sent_sender_mesh_index[0][:, part],
            sent_intersection_extent[0][:, part],
            sent_entry_tally[0] - chunk * width,
        )
        block = lax.all_to_all(values, ("lat", "lon"), split_axis=0, concat_axis=0, tiled=True)
        atmosphere = atmosphere + spread_cells(block, received_atmosphere_mesh_index[0][:, part], ACELL)
    return (height, east, north, tracer_new, atmosphere)


def solution(mesh):
    in_specs = (
        P("lat", "lon"),
        P("lat", "lon"),
        P("lat", "lon"),
        P("lat", "lon"),
        P(None, "lat", "lon"),
        P(None, "lat", "lon"),
        P(None, "lat", "lon"),
        P(("lat", "lon"), None, None),
        P(("lat", "lon"), None, None),
        P(("lat", "lon"), None),
        P(("lat", "lon"), None, None),
    )
    out_specs = (
        P("lat", "lon"),
        P("lat", "lon"),
        P("lat", "lon"),
        P(None, "lat", "lon"),
        P(None, ("lat", "lon")),
    )
    return jax.shard_map(local, mesh=mesh, in_specs=in_specs, out_specs=out_specs, check_vma=False)
```

```python
import functools
import math

import jax
import jax.numpy as jnp
from jax import lax
from jax.experimental import pallas as pl
from jax.sharding import PartitionSpec as P

VERTICAL_STRATA = 8
STEPS = 4
NF = 4
ACELL = 4096


mass_coef = 0.7
slope_coef = 0.7
spin_coef = 0.3
mix_coef = 0.1
carry_coef = 0.1


HALO = 2 * STEPS


def exchange(block, signs, width):
    planes, rows, columns = block.shape
    sectors = lax.axis_size("lon")
    bands = lax.axis_size("lat")
    eastward = [(i, (i + 1) % sectors) for i in range(sectors)]
    westward = [((i + 1) % sectors, i) for i in range(sectors)]
    from_west = lax.ppermute(block[:, :, columns - width :], "lon", eastward)
    from_east = lax.ppermute(block[:, :, :width], "lon", westward)
    wide = jnp.concatenate([from_west, block, from_east], axis=2)
    upward = [(b, b + 1) for b in range(bands - 1)]
    downward = [(b + 1, b) for b in range(bands - 1)]
    top = wide[:, rows - width :, :]
    from_south = lax.ppermute(top, "lat", upward)
    from_north = lax.ppermute(wide[:, :width, :], "lat", downward)
    last = (bands - 1) * sectors
    mirror = [(last + j, last + sectors - 1 - j) for j in range(sectors)]
    folded = lax.ppermute(top, ("lat", "lon"), mirror)
    folded = jnp.flip(folded, axis=(1, 2)) * signs[:, None, None]
    on_top = lax.axis_index("lat") == bands - 1
    north_rim = jnp.where(on_top, folded, from_north)
    return jnp.concatenate([from_south, wide, north_rim], axis=1)


def east_of(x):
    return jnp.concatenate([x[..., 1:], x[..., -1:]], axis=-1)


def west_of(x):
    return jnp.concatenate([x[..., :1], x[..., :-1]], axis=-1)


def north_of(x):
    return jnp.concatenate([x[..., 1:, :], x[..., -1:, :]], axis=-2)


def south_of(x):
    return jnp.concatenate([x[..., :1, :], x[..., :-1, :]], axis=-2)


GROUP = 32
CHUNKS = 2


def split_pieces(x):
    high = x.astype(jnp.bfloat16)
    low = (x - high.astype(jnp.float32)).astype(jnp.bfloat16)
    return high, low


def pick_kernel(offset, table_ref, index_ref, extent_ref, tally_ref, out_ref):
    fields_count = out_ref.shape[1]
    slots = index_ref.shape[1]
    table_rows = table_ref.shape[0]
    columns = table_ref.shape[1]
    rows = table_rows // fields_count
    table = jnp.concatenate(split_pieces(table_ref[...]), axis=1)
    column_ids = lax.broadcasted_iota(jnp.int32, (columns, slots), 0)
    row_ids = lax.broadcasted_iota(jnp.int32, (8, slots), 0)
    slot_ids = lax.broadcasted_iota(jnp.int32, (1, slots), 1) + offset
    for owner in range(index_ref.shape[0]):
        index = index_ref[pl.ds(owner, 1), :]
        hot = (column_ids == index % columns).astype(jnp.bfloat16)
        by_column = jnp.dot(
            table, jnp.concatenate([hot, hot], axis=0), preferred_element_type=jnp.float32
        )
        row = index // columns
        masks = [row_ids + 8 * tile == row for tile in range(rows // 8)]
        weight = jnp.where(
            slot_ids < tally_ref[pl.ds(owner, 1), :], extent_ref[pl.ds(owner, 1), :], 0.0
        )
        for field in range(fields_count):
            chosen = jnp.zeros((8, slots), jnp.float32)
            for tile in range(rows // 8):
                start = field * rows + tile * 8
                chosen = jnp.where(masks[tile], by_column[start : start + 8], chosen)
            picked = jnp.sum(chosen, axis=0, keepdims=True)
            out_ref[owner, pl.ds(field, 1), :] = picked * weight


def pick_cells(surface_grid, indices, extent, tally, chunk, slots):
    fields_count, rows, columns = surface_grid.shape
    owners = indices.shape[0]
    table = surface_grid.reshape(fields_count * rows, columns)
    return pl.pallas_call(
        functools.partial(pick_kernel, chunk * slots),
        out_shape=jax.ShapeDtypeStruct((owners, fields_count, slots), jnp.float32),
        grid=(owners // GROUP,),
        in_specs=[
            pl.BlockSpec((fields_count * rows, columns), lambda i: (0, 0)),
            pl.BlockSpec((GROUP, slots), lambda i: (i, chunk)),
            pl.BlockSpec((GROUP, slots), lambda i: (i, chunk)),
            pl.BlockSpec((GROUP, 1), lambda i: (i, 0)),
        ],
        out_specs=pl.BlockSpec((GROUP, fields_count, slots), lambda i: (i, 0, 0)),
    )(table, indices, extent, tally[:, None])


def spread_kernel(value_ref, target_ref, start_ref, out_ref):
    fields_count = value_ref.shape[1]
    slots = value_ref.shape[2]
    lows = out_ref.shape[0]
    highs = out_ref.shape[1] // (2 * fields_count)

    @pl.when(pl.program_id(0) == 0)
    def _():
        out_ref[...] = start_ref[...]

    high_ids = lax.broadcasted_iota(jnp.int32, (highs, slots), 0)
    low_ids = lax.broadcasted_iota(jnp.int32, (lows, slots), 0)
    total = jnp.zeros(out_ref.shape, jnp.float32)
    for sender in range(target_ref.shape[0]):
        target = target_ref[pl.ds(sender, 1), :]
        high_hot = high_ids == target // lows
        low_hot = (low_ids == target % lows).astype(jnp.bfloat16)
        pieces = []
        for field in range(fields_count):
            high, low_part = split_pieces(value_ref[sender, pl.ds(field, 1), :])
            pieces.append((high, low_part))
        weighted = jnp.concatenate(
            [
                jnp.where(high_hot, pieces[field][part].astype(jnp.float32), 0.0).astype(jnp.bfloat16)
                for part in range(2)
                for field in range(fields_count)
            ],
            axis=0,
        )
        total = total + lax.dot_general(
            low_hot, weighted, (((1,), (1,)), ((), ())), preferred_element_type=jnp.float32
        )
    out_ref[...] += total


SPREAD_LOWS = 128


def spread_cells(values, targets, chunk, start):
    senders, fields_count, slots = values.shape
    shape = start.shape
    return pl.pallas_call(
        spread_kernel,
        out_shape=jax.ShapeDtypeStruct(shape, jnp.float32),
        grid=(senders // GROUP,),
        in_specs=[
            pl.BlockSpec((GROUP, fields_count, slots), lambda i: (i, 0, 0)),
            pl.BlockSpec((GROUP, slots), lambda i: (i, chunk)),
            pl.BlockSpec(shape, lambda i: (0, 0)),
        ],
        out_specs=pl.BlockSpec(shape, lambda i: (0, 0)),
        input_output_aliases={2: 0},
    )(values, targets, start)


def local(
    starting_sea_elevation,
    zonal_integrated_flux,
    meridional_integrated_flux,
    ocean_strata_total,
    thermal_anomaly,
    zonal_baroclinic_velocity,
    meridional_baroclinic_velocity,
    sent_sender_mesh_index,
    sent_intersection_extent,
    sent_entry_tally,
    received_atmosphere_mesh_index,
):
    band_rows, band_columns = starting_sea_elevation.shape
    grid_rows = band_rows * lax.axis_size("lat")
    band = lax.axis_index("lat")
    depth = ocean_strata_total.astype(jnp.float32)
    planes = jnp.concatenate(
        [
            jnp.stack([starting_sea_elevation, zonal_integrated_flux, meridional_integrated_flux, depth]),
            thermal_anomaly,
        ],
        axis=0,
    )
    signs = jnp.array([1.0, -1.0, -1.0] + [1.0] * (1 + VERTICAL_STRATA), jnp.float32)
    ext = exchange(planes, signs, HALO)
    depth_ext = ext[3]
    wet = (depth_ext > 0).astype(jnp.float32)
    hnorm = depth_ext / VERTICAL_STRATA
    height = ext[0] * wet
    east = ext[1] * wet
    north = ext[2] * wet
    global_rows = band * band_rows - HALO + jnp.arange(band_rows + 2 * HALO)
    global_rows = jnp.where(global_rows >= grid_rows, 2 * grid_rows - 1 - global_rows, global_rows)
    rows = global_rows.astype(jnp.float32)
    rotation = (-spin_coef * jnp.cos(jnp.pi * (rows + 0.5) / grid_rows))[:, None]
    for step in range(STEPS):
        height = wet * (height - mass_coef * (east_of(east) - west_of(east) + (north_of(north) - south_of(north))))
        east = wet * (east - slope_coef * hnorm * (east_of(height) - west_of(height)) + rotation * north)
        north = wet * (north - slope_coef * hnorm * (north_of(height) - south_of(height)) - rotation * east)
    inner = (slice(HALO, HALO + band_rows), slice(HALO, HALO + band_columns))
    height = height[inner]
    east = east[inner]
    north = north[inner]
    near = (slice(None), slice(HALO - 1, HALO + band_rows + 1), slice(HALO - 1, HALO + band_columns + 1))
    levels_float = jnp.arange(VERTICAL_STRATA).astype(jnp.float32)[:, None, None]
    wet_wide = (levels_float < depth_ext[None][near]).astype(jnp.float32)
    tracer_wide = ext[4:][near] * wet_wide
    centre = (slice(None), slice(1, -1), slice(1, -1))
    submerged_stratum_mask = wet_wide[centre]
    passive_scalar_values = tracer_wide[centre]
    tracer_e = east_of(tracer_wide)[centre]
    tracer_w = west_of(tracer_wide)[centre]
    tracer_n = north_of(tracer_wide)[centre]
    tracer_s = south_of(tracer_wide)[centre]
    wet_e = east_of(wet_wide)[centre]
    wet_w = west_of(wet_wide)[centre]
    wet_n = north_of(wet_wide)[centre]
    wet_s = south_of(wet_wide)[centre]
    mixing = (
        wet_e * (tracer_e - passive_scalar_values)
        + wet_w * (tracer_w - passive_scalar_values)
        + wet_n * (tracer_n - passive_scalar_values)
        + wet_s * (tracer_s - passive_scalar_values)
    )
    speed_east = east[None] + zonal_baroclinic_velocity
    speed_north = north[None] + meridional_baroclinic_velocity
    carried = speed_east * (tracer_e - tracer_w) + speed_north * (tracer_n - tracer_s)
    tracer_new = submerged_stratum_mask * (
        passive_scalar_values + mix_coef * mixing - carry_coef * carried
    )
    surface_grid = jnp.stack([height, speed_east[0], speed_north[0], tracer_new[0]])
    slots = sent_sender_mesh_index.shape[2]
    width = slots // CHUNKS
    highs = ACELL // SPREAD_LOWS
    summed = jnp.zeros((SPREAD_LOWS, 2 * NF * highs), jnp.float32)
    for chunk in range(CHUNKS):
        values = pick_cells(
            surface_grid,
            sent_sender_mesh_index[0],
            sent_intersection_extent[0],
            sent_entry_tally[0],
            chunk,
            width,
        )
        block = lax.all_to_all(values, ("lat", "lon"), split_axis=0, concat_axis=0, tiled=True)
        summed = spread_cells(block, received_atmosphere_mesh_index[0], chunk, summed)
    summed = summed.reshape(SPREAD_LOWS, 2, NF, highs).sum(axis=1)
    atmosphere = jnp.transpose(summed, (1, 2, 0)).reshape(NF, ACELL)
    return (height, east, north, tracer_new, atmosphere)


def solution(mesh):
    in_specs = (
        P("lat", "lon"),
        P("lat", "lon"),
        P("lat", "lon"),
        P("lat", "lon"),
        P(None, "lat", "lon"),
        P(None, "lat", "lon"),
        P(None, "lat", "lon"),
        P(("lat", "lon"), None, None),
        P(("lat", "lon"), None, None),
        P(("lat", "lon"), None),
        P(("lat", "lon"), None, None),
    )
    out_specs = (
        P("lat", "lon"),
        P("lat", "lon"),
        P("lat", "lon"),
        P(None, "lat", "lon"),
        P(None, ("lat", "lon")),
    )
    return jax.shard_map(local, mesh=mesh, in_specs=in_specs, out_specs=out_specs, check_vma=False)
```

```python
import functools
import math

import jax
import jax.numpy as jnp
from jax import lax
from jax.experimental import pallas as pl
from jax.sharding import PartitionSpec as P

VERTICAL_STRATA = 8
STEPS = 4
NF = 4
ACELL = 4096


mass_coef = 0.7
slope_coef = 0.7
spin_coef = 0.3
mix_coef = 0.1
carry_coef = 0.1


HALO = 2 * STEPS


def exchange(block, signs, width):
    planes, rows, columns = block.shape
    sectors = lax.axis_size("lon")
    bands = lax.axis_size("lat")
    eastward = [(i, (i + 1) % sectors) for i in range(sectors)]
    westward = [((i + 1) % sectors, i) for i in range(sectors)]
    from_west = lax.ppermute(block[:, :, columns - width :], "lon", eastward)
    from_east = lax.ppermute(block[:, :, :width], "lon", westward)
    wide = jnp.concatenate([from_west, block, from_east], axis=2)
    upward = [(b, b + 1) for b in range(bands - 1)]
    downward = [(b + 1, b) for b in range(bands - 1)]
    top = wide[:, rows - width :, :]
    from_south = lax.ppermute(top, "lat", upward)
    from_north = lax.ppermute(wide[:, :width, :], "lat", downward)
    last = (bands - 1) * sectors
    mirror = [(last + j, last + sectors - 1 - j) for j in range(sectors)]
    folded = lax.ppermute(top, ("lat", "lon"), mirror)
    folded = jnp.flip(folded, axis=(1, 2)) * signs[:, None, None]
    on_top = lax.axis_index("lat") == bands - 1
    north_rim = jnp.where(on_top, folded, from_north)
    return jnp.concatenate([from_south, wide, north_rim], axis=1)


def east_of(x):
    return jnp.concatenate([x[..., 1:], x[..., -1:]], axis=-1)


def west_of(x):
    return jnp.concatenate([x[..., :1], x[..., :-1]], axis=-1)


def north_of(x):
    return jnp.concatenate([x[..., 1:, :], x[..., -1:, :]], axis=-2)


def south_of(x):
    return jnp.concatenate([x[..., :1, :], x[..., :-1, :]], axis=-2)


GROUP = 32
CHUNKS = 2


def split_pieces(x):
    high = x.astype(jnp.bfloat16)
    low = (x - high.astype(jnp.float32)).astype(jnp.bfloat16)
    return high, low


def pick_kernel(offset, table_ref, index_ref, extent_ref, tally_ref, out_ref):
    fields_count = out_ref.shape[1]
    slots = index_ref.shape[1]
    table_rows = table_ref.shape[0]
    columns = table_ref.shape[1]
    rows = table_rows // fields_count
    table = jnp.concatenate(split_pieces(table_ref[...]), axis=1)
    column_ids = lax.broadcasted_iota(jnp.int32, (columns, slots), 0)
    row_ids = lax.broadcasted_iota(jnp.int32, (8, slots), 0)
    slot_ids = lax.broadcasted_iota(jnp.int32, (1, slots), 1) + offset
    for owner in range(index_ref.shape[0]):
        index = index_ref[pl.ds(owner, 1), :]
        hot = (column_ids == index % columns).astype(jnp.bfloat16)
        by_column = jnp.dot(
            table, jnp.concatenate([hot, hot], axis=0), preferred_element_type=jnp.float32
        )
        row = index // columns
        masks = [row_ids + 8 * tile == row for tile in range(rows // 8)]
        weight = jnp.where(
            slot_ids < tally_ref[pl.ds(owner, 1), :], extent_ref[pl.ds(owner, 1), :], 0.0
        )
        for field in range(fields_count):
            chosen = jnp.zeros((8, slots), jnp.float32)
            for tile in range(rows // 8):
                start = field * rows + tile * 8
                chosen = jnp.where(masks[tile], by_column[start : start + 8], chosen)
            picked = jnp.sum(chosen, axis=0, keepdims=True)
            out_ref[owner, pl.ds(field, 1), :] = picked * weight


def pick_cells(surface_grid, indices, extent, tally, chunk, slots):
    fields_count, rows, columns = surface_grid.shape
    owners = indices.shape[0]
    table = surface_grid.reshape(fields_count * rows, columns)
    return pl.pallas_call(
        functools.partial(pick_kernel, chunk * slots),
        out_shape=jax.ShapeDtypeStruct((owners, fields_count, slots), jnp.float32),
        grid=(owners // GROUP,),
        in_specs=[
            pl.BlockSpec((fields_count * rows, columns), lambda i: (0, 0)),
            pl.BlockSpec((GROUP, slots), lambda i: (i, chunk)),
            pl.BlockSpec((GROUP, slots), lambda i: (i, chunk)),
            pl.BlockSpec((GROUP, 1), lambda i: (i, 0)),
        ],
        out_specs=pl.BlockSpec((GROUP, fields_count, slots), lambda i: (i, 0, 0)),
    )(table, indices, extent, tally[:, None])


def spread_kernel(value_ref, target_ref, start_ref, out_ref):
    fields_count = value_ref.shape[1]
    slots = value_ref.shape[2]
    lows = out_ref.shape[1]
    highs = out_ref.shape[0] // (2 * fields_count)

    @pl.when(pl.program_id(0) == 0)
    def _():
        out_ref[...] = start_ref[...]

    high_ids = lax.broadcasted_iota(jnp.int32, (highs, slots), 0)
    low_ids = lax.broadcasted_iota(jnp.int32, (lows, slots), 0)
    total = jnp.zeros(out_ref.shape, jnp.float32)
    for sender in range(target_ref.shape[0]):
        target = target_ref[pl.ds(sender, 1), :]
        high_hot = high_ids == target // lows
        low_hot = (low_ids == target % lows).astype(jnp.bfloat16)
        pieces = []
        for field in range(fields_count):
            high, low_part = split_pieces(value_ref[sender, pl.ds(field, 1), :])
            pieces.append((high, low_part))
        weighted = jnp.concatenate(
            [
                jnp.where(high_hot, pieces[field][part].astype(jnp.float32), 0.0).astype(jnp.bfloat16)
                for part in range(2)
                for field in range(fields_count)
            ],
            axis=0,
        )
        total = total + lax.dot_general(
            weighted, low_hot, (((1,), (1,)), ((), ())), preferred_element_type=jnp.float32
        )
    out_ref[...] += total


SPREAD_LOWS = 128


def spread_cells(values, targets, chunk, start):
    senders, fields_count, slots = values.shape
    shape = start.shape
    return pl.pallas_call(
        spread_kernel,
        out_shape=jax.ShapeDtypeStruct(shape, jnp.float32),
        grid=(senders // GROUP,),
        in_specs=[
            pl.BlockSpec((GROUP, fields_count, slots), lambda i: (i, 0, 0)),
            pl.BlockSpec((GROUP, slots), lambda i: (i, chunk)),
            pl.BlockSpec(shape, lambda i: (0, 0)),
        ],
        out_specs=pl.BlockSpec(shape, lambda i: (0, 0)),
        input_output_aliases={2: 0},
    )(values, targets, start)


def local(
    starting_sea_elevation,
    zonal_integrated_flux,
    meridional_integrated_flux,
    ocean_strata_total,
    thermal_anomaly,
    zonal_baroclinic_velocity,
    meridional_baroclinic_velocity,
    sent_sender_mesh_index,
    sent_intersection_extent,
    sent_entry_tally,
    received_atmosphere_mesh_index,
):
    band_rows, band_columns = starting_sea_elevation.shape
    grid_rows = band_rows * lax.axis_size("lat")
    band = lax.axis_index("lat")
    depth = ocean_strata_total.astype(jnp.float32)
    planes = jnp.concatenate(
        [
            jnp.stack([starting_sea_elevation, zonal_integrated_flux, meridional_integrated_flux, depth]),
            thermal_anomaly,
        ],
        axis=0,
    )
    signs = jnp.array([1.0, -1.0, -1.0] + [1.0] * (1 + VERTICAL_STRATA), jnp.float32)
    ext = exchange(planes, signs, HALO)
    depth_ext = ext[3]
    wet = (depth_ext > 0).astype(jnp.float32)
    hnorm = depth_ext / VERTICAL_STRATA
    height = ext[0] * wet
    east = ext[1] * wet
    north = ext[2] * wet
    global_rows = band * band_rows - HALO + jnp.arange(band_rows + 2 * HALO)
    global_rows = jnp.where(global_rows >= grid_rows, 2 * grid_rows - 1 - global_rows, global_rows)
    rows = global_rows.astype(jnp.float32)
    rotation = (-spin_coef * jnp.cos(jnp.pi * (rows + 0.5) / grid_rows))[:, None]
    for step in range(STEPS):
        height = wet * (height - mass_coef * (east_of(east) - west_of(east) + (north_of(north) - south_of(north))))
        east = wet * (east - slope_coef * hnorm * (east_of(height) - west_of(height)) + rotation * north)
        north = wet * (north - slope_coef * hnorm * (north_of(height) - south_of(height)) - rotation * east)
    inner = (slice(HALO, HALO + band_rows), slice(HALO, HALO + band_columns))
    height = height[inner]
    east = east[inner]
    north = north[inner]
    near = (slice(None), slice(HALO - 1, HALO + band_rows + 1), slice(HALO - 1, HALO + band_columns + 1))
    levels_float = jnp.arange(VERTICAL_STRATA).astype(jnp.float32)[:, None, None]
    wet_wide = (levels_float < depth_ext[None][near]).astype(jnp.float32)
    tracer_wide = ext[4:][near] * wet_wide
    centre = (slice(None), slice(1, -1), slice(1, -1))
    submerged_stratum_mask = wet_wide[centre]
    passive_scalar_values = tracer_wide[centre]
    tracer_e = east_of(tracer_wide)[centre]
    tracer_w = west_of(tracer_wide)[centre]
    tracer_n = north_of(tracer_wide)[centre]
    tracer_s = south_of(tracer_wide)[centre]
    wet_e = east_of(wet_wide)[centre]
    wet_w = west_of(wet_wide)[centre]
    wet_n = north_of(wet_wide)[centre]
    wet_s = south_of(wet_wide)[centre]
    mixing = (
        wet_e * (tracer_e - passive_scalar_values)
        + wet_w * (tracer_w - passive_scalar_values)
        + wet_n * (tracer_n - passive_scalar_values)
        + wet_s * (tracer_s - passive_scalar_values)
    )
    speed_east = east[None] + zonal_baroclinic_velocity
    speed_north = north[None] + meridional_baroclinic_velocity
    carried = speed_east * (tracer_e - tracer_w) + speed_north * (tracer_n - tracer_s)
    tracer_new = submerged_stratum_mask * (
        passive_scalar_values + mix_coef * mixing - carry_coef * carried
    )
    surface_grid = jnp.stack([height, speed_east[0], speed_north[0], tracer_new[0]])
    slots = sent_sender_mesh_index.shape[2]
    width = slots // CHUNKS
    highs = ACELL // SPREAD_LOWS
    summed = jnp.zeros((2 * NF * highs, SPREAD_LOWS), jnp.float32)
    for chunk in range(CHUNKS):
        values = pick_cells(
            surface_grid,
            sent_sender_mesh_index[0],
            sent_intersection_extent[0],
            sent_entry_tally[0],
            chunk,
            width,
        )
        block = lax.all_to_all(values, ("lat", "lon"), split_axis=0, concat_axis=0, tiled=True)
        summed = spread_cells(block, received_atmosphere_mesh_index[0], chunk, summed)
    atmosphere = summed.reshape(2, NF, ACELL).sum(axis=0)
    return (height, east, north, tracer_new, atmosphere)


def solution(mesh):
    in_specs = (
        P("lat", "lon"),
        P("lat", "lon"),
        P("lat", "lon"),
        P("lat", "lon"),
        P(None, "lat", "lon"),
        P(None, "lat", "lon"),
        P(None, "lat", "lon"),
        P(("lat", "lon"), None, None),
        P(("lat", "lon"), None, None),
        P(("lat", "lon"), None),
        P(("lat", "lon"), None, None),
    )
    out_specs = (
        P("lat", "lon"),
        P("lat", "lon"),
        P("lat", "lon"),
        P(None, "lat", "lon"),
        P(None, ("lat", "lon")),
    )
    return jax.shard_map(local, mesh=mesh, in_specs=in_specs, out_specs=out_specs, check_vma=False)
```

```python
import functools
import math

import jax
import jax.numpy as jnp
from jax import lax
from jax.experimental import pallas as pl
from jax.experimental.pallas import tpu as pltpu
from jax.sharding import PartitionSpec as P

VERTICAL_STRATA = 8
STEPS = 4
NF = 4
ACELL = 4096


mass_coef = 0.7
slope_coef = 0.7
spin_coef = 0.3
mix_coef = 0.1
carry_coef = 0.1


HALO = 2 * STEPS


def exchange(block, signs, width):
    planes, rows, columns = block.shape
    sectors = lax.axis_size("lon")
    bands = lax.axis_size("lat")
    eastward = [(i, (i + 1) % sectors) for i in range(sectors)]
    westward = [((i + 1) % sectors, i) for i in range(sectors)]
    from_west = lax.ppermute(block[:, :, columns - width :], "lon", eastward)
    from_east = lax.ppermute(block[:, :, :width], "lon", westward)
    wide = jnp.concatenate([from_west, block, from_east], axis=2)
    upward = [(b, b + 1) for b in range(bands - 1)]
    downward = [(b + 1, b) for b in range(bands - 1)]
    top = wide[:, rows - width :, :]
    from_south = lax.ppermute(top, "lat", upward)
    from_north = lax.ppermute(wide[:, :width, :], "lat", downward)
    last = (bands - 1) * sectors
    mirror = [(last + j, last + sectors - 1 - j) for j in range(sectors)]
    folded = lax.ppermute(top, ("lat", "lon"), mirror)
    folded = jnp.flip(folded, axis=(1, 2)) * signs[:, None, None]
    on_top = lax.axis_index("lat") == bands - 1
    north_rim = jnp.where(on_top, folded, from_north)
    return jnp.concatenate([from_south, wide, north_rim], axis=1)


def east_of(x):
    return jnp.concatenate([x[..., 1:], x[..., -1:]], axis=-1)


def west_of(x):
    return jnp.concatenate([x[..., :1], x[..., :-1]], axis=-1)


def north_of(x):
    return jnp.concatenate([x[..., 1:, :], x[..., -1:, :]], axis=-2)


def south_of(x):
    return jnp.concatenate([x[..., :1, :], x[..., :-1, :]], axis=-2)


GROUP = 32
CHUNKS = 2


def split_pieces(x):
    high = x.astype(jnp.bfloat16)
    low = (x - high.astype(jnp.float32)).astype(jnp.bfloat16)
    return high, low


def pick_kernel(offset, table_ref, index_ref, extent_ref, tally_ref, out_ref):
    fields_count = out_ref.shape[1]
    slots = index_ref.shape[1]
    table_rows = table_ref.shape[0]
    columns = table_ref.shape[1]
    rows = table_rows // fields_count
    table = jnp.concatenate(split_pieces(table_ref[...]), axis=1)
    column_ids = lax.broadcasted_iota(jnp.int32, (columns, slots), 0)
    row_ids = lax.broadcasted_iota(jnp.int32, (8, slots), 0)
    slot_ids = lax.broadcasted_iota(jnp.int32, (1, slots), 1) + offset
    for owner in range(index_ref.shape[0]):
        index = index_ref[pl.ds(owner, 1), :]
        hot = (column_ids == index % columns).astype(jnp.bfloat16)
        by_column = jnp.dot(
            table, jnp.concatenate([hot, hot], axis=0), preferred_element_type=jnp.float32
        )
        row = index // columns
        masks = [row_ids + 8 * tile == row for tile in range(rows // 8)]
        weight = jnp.where(
            slot_ids < tally_ref[pl.ds(owner, 1), :], extent_ref[pl.ds(owner, 1), :], 0.0
        )
        for field in range(fields_count):
            chosen = jnp.zeros((8, slots), jnp.float32)
            for tile in range(rows // 8):
                start = field * rows + tile * 8
                chosen = jnp.where(masks[tile], by_column[start : start + 8], chosen)
            picked = jnp.sum(chosen, axis=0, keepdims=True)
            out_ref[owner, pl.ds(field, 1), :] = picked * weight


def pick_cells(surface_grid, indices, extent, tally, chunk, slots):
    fields_count, rows, columns = surface_grid.shape
    owners = indices.shape[0]
    table = surface_grid.reshape(fields_count * rows, columns)
    return pl.pallas_call(
        functools.partial(pick_kernel, chunk * slots),
        out_shape=jax.ShapeDtypeStruct((owners, fields_count, slots), jnp.float32),
        grid=(owners // GROUP,),
        in_specs=[
            pl.BlockSpec((fields_count * rows, columns), lambda i: (0, 0)),
            pl.BlockSpec((GROUP, slots), lambda i: (i, chunk)),
            pl.BlockSpec((GROUP, slots), lambda i: (i, chunk)),
            pl.BlockSpec((GROUP, 1), lambda i: (i, 0)),
        ],
        out_specs=pl.BlockSpec((GROUP, fields_count, slots), lambda i: (i, 0, 0)),
    )(table, indices, extent, tally[:, None])


def spread_kernel(has_start, final, value_ref, target_ref, *refs):
    if has_start:
        start_ref, refs = refs[0], refs[1:]
    out_ref = refs[0]
    acc_ref = refs[1] if final else out_ref
    fields_count = value_ref.shape[1]
    slots = value_ref.shape[2]
    lows = acc_ref.shape[1]
    highs = acc_ref.shape[0] // (2 * fields_count)

    @pl.when(pl.program_id(0) == 0)
    def _():
        if has_start:
            acc_ref[...] = start_ref[...]
        else:
            acc_ref[...] = jnp.zeros_like(acc_ref)

    high_ids = lax.broadcasted_iota(jnp.int32, (highs, slots), 0)
    low_ids = lax.broadcasted_iota(jnp.int32, (lows, slots), 0)
    total = jnp.zeros(acc_ref.shape, jnp.float32)
    for sender in range(target_ref.shape[0]):
        target = target_ref[pl.ds(sender, 1), :]
        high_hot = high_ids == target // lows
        low_hot = (low_ids == target % lows).astype(jnp.bfloat16)
        pieces = []
        for field in range(fields_count):
            high, low_part = split_pieces(value_ref[sender, pl.ds(field, 1), :])
            pieces.append((high, low_part))
        weighted = jnp.concatenate(
            [
                jnp.where(high_hot, pieces[field][part].astype(jnp.float32), 0.0).astype(jnp.bfloat16)
                for part in range(2)
                for field in range(fields_count)
            ],
            axis=0,
        )
        total = total + lax.dot_general(
            weighted, low_hot, (((1,), (1,)), ((), ())), preferred_element_type=jnp.float32
        )
    acc_ref[...] += total

    if final:

        @pl.when(pl.program_id(0) == pl.num_programs(0) - 1)
        def _():
            half = fields_count * highs
            for field in range(fields_count):
                for high in range(highs):
                    row = field * highs + high
                    out_ref[pl.ds(field, 1), pl.ds(high * lows, lows)] = (
                        acc_ref[pl.ds(row, 1), :] + acc_ref[pl.ds(half + row, 1), :]
                    )


SPREAD_LOWS = 128


def spread_cells(values, targets, chunk, start, final):
    senders, fields_count, slots = values.shape
    highs = ACELL // SPREAD_LOWS
    shape = (2 * fields_count * highs, SPREAD_LOWS)
    in_specs = [
        pl.BlockSpec((GROUP, fields_count, slots), lambda i: (i, 0, 0)),
        pl.BlockSpec((GROUP, slots), lambda i: (i, chunk)),
    ]
    operands = [values, targets]
    if start is not None:
        in_specs.append(pl.BlockSpec(shape, lambda i: (0, 0)))
        operands.append(start)
    out_shape = (fields_count, ACELL) if final else shape
    return pl.pallas_call(
        functools.partial(spread_kernel, start is not None, final),
        out_shape=jax.ShapeDtypeStruct(out_shape, jnp.float32),
        grid=(senders // GROUP,),
        in_specs=in_specs,
        out_specs=pl.BlockSpec(out_shape, lambda i: (0, 0)),
        scratch_shapes=[pltpu.VMEM(shape, jnp.float32)] if final else [],
    )(*operands)


def local(
    starting_sea_elevation,
    zonal_integrated_flux,
    meridional_integrated_flux,
    ocean_strata_total,
    thermal_anomaly,
    zonal_baroclinic_velocity,
    meridional_baroclinic_velocity,
    sent_sender_mesh_index,
    sent_intersection_extent,
    sent_entry_tally,
    received_atmosphere_mesh_index,
):
    band_rows, band_columns = starting_sea_elevation.shape
    grid_rows = band_rows * lax.axis_size("lat")
    band = lax.axis_index("lat")
    depth = ocean_strata_total.astype(jnp.float32)
    planes = jnp.concatenate(
        [
            jnp.stack([starting_sea_elevation, zonal_integrated_flux, meridional_integrated_flux, depth]),
            thermal_anomaly,
        ],
        axis=0,
    )
    signs = jnp.array([1.0, -1.0, -1.0] + [1.0] * (1 + VERTICAL_STRATA), jnp.float32)
    ext = exchange(planes, signs, HALO)
    depth_ext = ext[3]
    wet = (depth_ext > 0).astype(jnp.float32)
    hnorm = depth_ext / VERTICAL_STRATA
    height = ext[0] * wet
    east = ext[1] * wet
    north = ext[2] * wet
    global_rows = band * band_rows - HALO + jnp.arange(band_rows + 2 * HALO)
    global_rows = jnp.where(global_rows >= grid_rows, 2 * grid_rows - 1 - global_rows, global_rows)
    rows = global_rows.astype(jnp.float32)
    rotation = (-spin_coef * jnp.cos(jnp.pi * (rows + 0.5) / grid_rows))[:, None]
    for step in range(STEPS):
        height = wet * (height - mass_coef * (east_of(east) - west_of(east) + (north_of(north) - south_of(north))))
        east = wet * (east - slope_coef * hnorm * (east_of(height) - west_of(height)) + rotation * north)
        north = wet * (north - slope_coef * hnorm * (north_of(height) - south_of(height)) - rotation * east)
    inner = (slice(HALO, HALO + band_rows), slice(HALO, HALO + band_columns))
    height = height[inner]
    east = east[inner]
    north = north[inner]
    near = (slice(None), slice(HALO - 1, HALO + band_rows + 1), slice(HALO - 1, HALO + band_columns + 1))
    levels_float = jnp.arange(VERTICAL_STRATA).astype(jnp.float32)[:, None, None]
    wet_wide = (levels_float < depth_ext[None][near]).astype(jnp.float32)
    tracer_wide = ext[4:][near] * wet_wide
    centre = (slice(None), slice(1, -1), slice(1, -1))
    submerged_stratum_mask = wet_wide[centre]
    passive_scalar_values = tracer_wide[centre]
    tracer_e = east_of(tracer_wide)[centre]
    tracer_w = west_of(tracer_wide)[centre]
    tracer_n = north_of(tracer_wide)[centre]
    tracer_s = south_of(tracer_wide)[centre]
    wet_e = east_of(wet_wide)[centre]
    wet_w = west_of(wet_wide)[centre]
    wet_n = north_of(wet_wide)[centre]
    wet_s = south_of(wet_wide)[centre]
    mixing = (
        wet_e * (tracer_e - passive_scalar_values)
        + wet_w * (tracer_w - passive_scalar_values)
        + wet_n * (tracer_n - passive_scalar_values)
        + wet_s * (tracer_s - passive_scalar_values)
    )
    speed_east = east[None] + zonal_baroclinic_velocity
    speed_north = north[None] + meridional_baroclinic_velocity
    carried = speed_east * (tracer_e - tracer_w) + speed_north * (tracer_n - tracer_s)
    tracer_new = submerged_stratum_mask * (
        passive_scalar_values + mix_coef * mixing - carry_coef * carried
    )
    surface_grid = jnp.stack([height, speed_east[0], speed_north[0], tracer_new[0]])
    slots = sent_sender_mesh_index.shape[2]
    width = slots // CHUNKS
    summed = None
    for chunk in range(CHUNKS):
        values = pick_cells(
            surface_grid,
            sent_sender_mesh_index[0],
            sent_intersection_extent[0],
            sent_entry_tally[0],
            chunk,
            width,
        )
        block = lax.all_to_all(values, ("lat", "lon"), split_axis=0, concat_axis=0, tiled=True)
        summed = spread_cells(
            block, received_atmosphere_mesh_index[0], chunk, summed, chunk == CHUNKS - 1
        )
    atmosphere = summed
    return (height, east, north, tracer_new, atmosphere)


def solution(mesh):
    in_specs = (
        P("lat", "lon"),
        P("lat", "lon"),
        P("lat", "lon"),
        P("lat", "lon"),
        P(None, "lat", "lon"),
        P(None, "lat", "lon"),
        P(None, "lat", "lon"),
        P(("lat", "lon"), None, None),
        P(("lat", "lon"), None, None),
        P(("lat", "lon"), None),
        P(("lat", "lon"), None, None),
    )
    out_specs = (
        P("lat", "lon"),
        P("lat", "lon"),
        P("lat", "lon"),
        P(None, "lat", "lon"),
        P(None, ("lat", "lon")),
    )
    return jax.shard_map(local, mesh=mesh, in_specs=in_specs, out_specs=out_specs, check_vma=False)
```

```python
import functools
import math

import jax
import jax.numpy as jnp
from jax import lax
from jax.experimental import pallas as pl
from jax.experimental.pallas import tpu as pltpu
from jax.sharding import PartitionSpec as P

VERTICAL_STRATA = 8
STEPS = 4
NF = 4
ACELL = 4096


mass_coef = 0.7
slope_coef = 0.7
spin_coef = 0.3
mix_coef = 0.1
carry_coef = 0.1


HALO = 2 * STEPS


def exchange(parts, signs, width):
    planes, rows, columns = sum(part.shape[0] for part in parts), *parts[0].shape[1:]
    sectors = lax.axis_size("lon")
    bands = lax.axis_size("lat")

    def gather(rows_part, columns_part):
        return jnp.concatenate([part[:, rows_part, columns_part] for part in parts], axis=0)

    everything = slice(None)
    eastward = [(i, (i + 1) % sectors) for i in range(sectors)]
    westward = [((i + 1) % sectors, i) for i in range(sectors)]
    from_west = lax.ppermute(gather(everything, slice(columns - width, None)), "lon", eastward)
    from_east = lax.ppermute(gather(everything, slice(0, width)), "lon", westward)

    def band_rows(rows_part):
        return jnp.concatenate(
            [from_west[:, rows_part, :], gather(rows_part, everything), from_east[:, rows_part, :]],
            axis=2,
        )

    upward = [(b, b + 1) for b in range(bands - 1)]
    downward = [(b + 1, b) for b in range(bands - 1)]
    top = band_rows(slice(rows - width, None))
    from_south = lax.ppermute(top, "lat", upward)
    from_north = lax.ppermute(band_rows(slice(0, width)), "lat", downward)
    last = (bands - 1) * sectors
    mirror = [(last + j, last + sectors - 1 - j) for j in range(sectors)]
    folded = lax.ppermute(top, ("lat", "lon"), mirror)
    folded = jnp.flip(folded, axis=(1, 2)) * signs[:, None, None]
    on_top = lax.axis_index("lat") == bands - 1
    north_rim = jnp.where(on_top, folded, from_north)
    wide = jnp.concatenate([from_west, jnp.concatenate(parts, axis=0), from_east], axis=2)
    return jnp.concatenate([from_south, wide, north_rim], axis=1)


def east_of(x):
    return jnp.concatenate([x[..., 1:], x[..., -1:]], axis=-1)


def west_of(x):
    return jnp.concatenate([x[..., :1], x[..., :-1]], axis=-1)


def north_of(x):
    return jnp.concatenate([x[..., 1:, :], x[..., -1:, :]], axis=-2)


def south_of(x):
    return jnp.concatenate([x[..., :1, :], x[..., :-1, :]], axis=-2)


GROUP = 32
CHUNKS = 2


def split_pieces(x):
    high = x.astype(jnp.bfloat16)
    low = (x - high.astype(jnp.float32)).astype(jnp.bfloat16)
    return high, low


def pick_kernel(offset, table_ref, index_ref, extent_ref, tally_ref, out_ref):
    fields_count = out_ref.shape[1]
    slots = index_ref.shape[1]
    table_rows = table_ref.shape[0]
    columns = table_ref.shape[1]
    rows = table_rows // fields_count
    table = jnp.concatenate(split_pieces(table_ref[...]), axis=1)
    column_ids = lax.broadcasted_iota(jnp.int32, (columns, slots), 0)
    row_ids = lax.broadcasted_iota(jnp.int32, (8, slots), 0)
    slot_ids = lax.broadcasted_iota(jnp.int32, (1, slots), 1) + offset
    for owner in range(index_ref.shape[0]):
        index = index_ref[pl.ds(owner, 1), :]
        hot = (column_ids == index % columns).astype(jnp.bfloat16)
        by_column = jnp.dot(
            table, jnp.concatenate([hot, hot], axis=0), preferred_element_type=jnp.float32
        )
        row = index // columns
        masks = [row_ids + 8 * tile == row for tile in range(rows // 8)]
        weight = jnp.where(
            slot_ids < tally_ref[pl.ds(owner, 1), :], extent_ref[pl.ds(owner, 1), :], 0.0
        )
        for field in range(fields_count):
            chosen = jnp.zeros((8, slots), jnp.float32)
            for tile in range(rows // 8):
                start = field * rows + tile * 8
                chosen = jnp.where(masks[tile], by_column[start : start + 8], chosen)
            picked = jnp.sum(chosen, axis=0, keepdims=True)
            out_ref[owner, pl.ds(field, 1), :] = picked * weight


def pick_cells(surface_grid, indices, extent, tally, chunk, slots):
    fields_count, rows, columns = surface_grid.shape
    owners = indices.shape[0]
    table = surface_grid.reshape(fields_count * rows, columns)
    return pl.pallas_call(
        functools.partial(pick_kernel, chunk * slots),
        out_shape=jax.ShapeDtypeStruct((owners, fields_count, slots), jnp.float32),
        grid=(owners // GROUP,),
        in_specs=[
            pl.BlockSpec((fields_count * rows, columns), lambda i: (0, 0)),
            pl.BlockSpec((GROUP, slots), lambda i: (i, chunk)),
            pl.BlockSpec((GROUP, slots), lambda i: (i, chunk)),
            pl.BlockSpec((GROUP, 1), lambda i: (i, 0)),
        ],
        out_specs=pl.BlockSpec((GROUP, fields_count, slots), lambda i: (i, 0, 0)),
    )(table, indices, extent, tally[:, None])


def spread_kernel(has_start, final, value_ref, target_ref, *refs):
    if has_start:
        start_ref, refs = refs[0], refs[1:]
    out_ref = refs[0]
    acc_ref = refs[1] if final else out_ref
    fields_count = value_ref.shape[1]
    slots = value_ref.shape[2]
    lows = acc_ref.shape[1]
    highs = acc_ref.shape[0] // (2 * fields_count)

    @pl.when(pl.program_id(0) == 0)
    def _():
        if has_start:
            acc_ref[...] = start_ref[...]
        else:
            acc_ref[...] = jnp.zeros_like(acc_ref)

    high_ids = lax.broadcasted_iota(jnp.int32, (highs, slots), 0)
    low_ids = lax.broadcasted_iota(jnp.int32, (lows, slots), 0)
    total = jnp.zeros(acc_ref.shape, jnp.float32)
    for sender in range(target_ref.shape[0]):
        target = target_ref[pl.ds(sender, 1), :]
        high_hot = high_ids == target // lows
        low_hot = (low_ids == target % lows).astype(jnp.bfloat16)
        pieces = []
        for field in range(fields_count):
            high, low_part = split_pieces(value_ref[sender, pl.ds(field, 1), :])
            pieces.append((high, low_part))
        weighted = jnp.concatenate(
            [
                jnp.where(high_hot, pieces[field][part].astype(jnp.float32), 0.0).astype(jnp.bfloat16)
                for part in range(2)
                for field in range(fields_count)
            ],
            axis=0,
        )
        total = total + lax.dot_general(
            weighted, low_hot, (((1,), (1,)), ((), ())), preferred_element_type=jnp.float32
        )
    acc_ref[...] += total

    if final:

        @pl.when(pl.program_id(0) == pl.num_programs(0) - 1)
        def _():
            half = fields_count * highs
            for field in range(fields_count):
                for high in range(highs):
                    row = field * highs + high
                    out_ref[pl.ds(field, 1), pl.ds(high * lows, lows)] = (
                        acc_ref[pl.ds(row, 1), :] + acc_ref[pl.ds(half + row, 1), :]
                    )


SPREAD_LOWS = 128


def spread_cells(values, targets, chunk, start, final):
    senders, fields_count, slots = values.shape
    highs = ACELL // SPREAD_LOWS
    shape = (2 * fields_count * highs, SPREAD_LOWS)
    in_specs = [
        pl.BlockSpec((GROUP, fields_count, slots), lambda i: (i, 0, 0)),
        pl.BlockSpec((GROUP, slots), lambda i: (i, chunk)),
    ]
    operands = [values, targets]
    if start is not None:
        in_specs.append(pl.BlockSpec(shape, lambda i: (0, 0)))
        operands.append(start)
    out_shape = (fields_count, ACELL) if final else shape
    return pl.pallas_call(
        functools.partial(spread_kernel, start is not None, final),
        out_shape=jax.ShapeDtypeStruct(out_shape, jnp.float32),
        grid=(senders // GROUP,),
        in_specs=in_specs,
        out_specs=pl.BlockSpec(out_shape, lambda i: (0, 0)),
        scratch_shapes=[pltpu.VMEM(shape, jnp.float32)] if final else [],
    )(*operands)


def local(
    starting_sea_elevation,
    zonal_integrated_flux,
    meridional_integrated_flux,
    ocean_strata_total,
    thermal_anomaly,
    zonal_baroclinic_velocity,
    meridional_baroclinic_velocity,
    sent_sender_mesh_index,
    sent_intersection_extent,
    sent_entry_tally,
    received_atmosphere_mesh_index,
):
    band_rows, band_columns = starting_sea_elevation.shape
    grid_rows = band_rows * lax.axis_size("lat")
    band = lax.axis_index("lat")
    depth = ocean_strata_total.astype(jnp.float32)
    planes = [
        starting_sea_elevation[None],
        zonal_integrated_flux[None],
        meridional_integrated_flux[None],
        depth[None],
        thermal_anomaly,
    ]
    signs = jnp.array([1.0, -1.0, -1.0] + [1.0] * (1 + VERTICAL_STRATA), jnp.float32)
    ext = exchange(planes, signs, HALO)
    depth_ext = ext[3]
    wet = (depth_ext > 0).astype(jnp.float32)
    hnorm = depth_ext / VERTICAL_STRATA
    height = ext[0] * wet
    east = ext[1] * wet
    north = ext[2] * wet
    global_rows = band * band_rows - HALO + jnp.arange(band_rows + 2 * HALO)
    global_rows = jnp.where(global_rows >= grid_rows, 2 * grid_rows - 1 - global_rows, global_rows)
    rows = global_rows.astype(jnp.float32)
    rotation = (-spin_coef * jnp.cos(jnp.pi * (rows + 0.5) / grid_rows))[:, None]
    for step in range(STEPS):
        height = wet * (height - mass_coef * (east_of(east) - west_of(east) + (north_of(north) - south_of(north))))
        east = wet * (east - slope_coef * hnorm * (east_of(height) - west_of(height)) + rotation * north)
        north = wet * (north - slope_coef * hnorm * (north_of(height) - south_of(height)) - rotation * east)
    inner = (slice(HALO, HALO + band_rows), slice(HALO, HALO + band_columns))
    height = height[inner]
    east = east[inner]
    north = north[inner]
    near = (slice(None), slice(HALO - 1, HALO + band_rows + 1), slice(HALO - 1, HALO + band_columns + 1))
    levels_float = jnp.arange(VERTICAL_STRATA).astype(jnp.float32)[:, None, None]
    wet_wide = (levels_float < depth_ext[None][near]).astype(jnp.float32)
    tracer_wide = ext[4:][near] * wet_wide
    centre = (slice(None), slice(1, -1), slice(1, -1))
    submerged_stratum_mask = wet_wide[centre]
    passive_scalar_values = tracer_wide[centre]
    tracer_e = east_of(tracer_wide)[centre]
    tracer_w = west_of(tracer_wide)[centre]
    tracer_n = north_of(tracer_wide)[centre]
    tracer_s = south_of(tracer_wide)[centre]
    wet_e = east_of(wet_wide)[centre]
    wet_w = west_of(wet_wide)[centre]
    wet_n = north_of(wet_wide)[centre]
    wet_s = south_of(wet_wide)[centre]
    mixing = (
        wet_e * (tracer_e - passive_scalar_values)
        + wet_w * (tracer_w - passive_scalar_values)
        + wet_n * (tracer_n - passive_scalar_values)
        + wet_s * (tracer_s - passive_scalar_values)
    )
    speed_east = east[None] + zonal_baroclinic_velocity
    speed_north = north[None] + meridional_baroclinic_velocity
    carried = speed_east * (tracer_e - tracer_w) + speed_north * (tracer_n - tracer_s)
    tracer_new = submerged_stratum_mask * (
        passive_scalar_values + mix_coef * mixing - carry_coef * carried
    )
    surface_grid = jnp.stack([height, speed_east[0], speed_north[0], tracer_new[0]])
    slots = sent_sender_mesh_index.shape[2]
    width = slots // CHUNKS
    summed = None
    for chunk in range(CHUNKS):
        values = pick_cells(
            surface_grid,
            sent_sender_mesh_index[0],
            sent_intersection_extent[0],
            sent_entry_tally[0],
            chunk,
            width,
        )
        block = lax.all_to_all(values, ("lat", "lon"), split_axis=0, concat_axis=0, tiled=True)
        summed = spread_cells(
            block, received_atmosphere_mesh_index[0], chunk, summed, chunk == CHUNKS - 1
        )
    atmosphere = summed
    return (height, east, north, tracer_new, atmosphere)


def solution(mesh):
    in_specs = (
        P("lat", "lon"),
        P("lat", "lon"),
        P("lat", "lon"),
        P("lat", "lon"),
        P(None, "lat", "lon"),
        P(None, "lat", "lon"),
        P(None, "lat", "lon"),
        P(("lat", "lon"), None, None),
        P(("lat", "lon"), None, None),
        P(("lat", "lon"), None),
        P(("lat", "lon"), None, None),
    )
    out_specs = (
        P("lat", "lon"),
        P("lat", "lon"),
        P("lat", "lon"),
        P(None, "lat", "lon"),
        P(None, ("lat", "lon")),
    )
    return jax.shard_map(local, mesh=mesh, in_specs=in_specs, out_specs=out_specs, check_vma=False)
```

```python
import functools
import math

import jax
import jax.numpy as jnp
from jax import lax
from jax.experimental import pallas as pl
from jax.experimental.pallas import tpu as pltpu
from jax.sharding import PartitionSpec as P

VERTICAL_STRATA = 8
STEPS = 4
NF = 4
ACELL = 4096


mass_coef = 0.7
slope_coef = 0.7
spin_coef = 0.3
mix_coef = 0.1
carry_coef = 0.1


HALO = 2 * STEPS


def exchange(block, signs, width):
    planes, rows, columns = block.shape
    sectors = lax.axis_size("lon")
    bands = lax.axis_size("lat")
    eastward = [(i, (i + 1) % sectors) for i in range(sectors)]
    westward = [((i + 1) % sectors, i) for i in range(sectors)]
    from_west = lax.ppermute(block[:, :, columns - width :], "lon", eastward)
    from_east = lax.ppermute(block[:, :, :width], "lon", westward)
    wide = jnp.concatenate([from_west, block, from_east], axis=2)
    upward = [(b, b + 1) for b in range(bands - 1)]
    downward = [(b + 1, b) for b in range(bands - 1)]
    top = wide[:, rows - width :, :]
    from_south = lax.ppermute(top, "lat", upward)
    from_north = lax.ppermute(wide[:, :width, :], "lat", downward)
    last = (bands - 1) * sectors
    mirror = [(last + j, last + sectors - 1 - j) for j in range(sectors)]
    folded = lax.ppermute(top, ("lat", "lon"), mirror)
    folded = jnp.flip(folded, axis=(1, 2)) * signs[:, None, None]
    on_top = lax.axis_index("lat") == bands - 1
    north_rim = jnp.where(on_top, folded, from_north)
    return jnp.concatenate([from_south, wide, north_rim], axis=1)


def east_of(x):
    return jnp.concatenate([x[..., 1:], x[..., -1:]], axis=-1)


def west_of(x):
    return jnp.concatenate([x[..., :1], x[..., :-1]], axis=-1)


def north_of(x):
    return jnp.concatenate([x[..., 1:, :], x[..., -1:, :]], axis=-2)


def south_of(x):
    return jnp.concatenate([x[..., :1, :], x[..., :-1, :]], axis=-2)


GROUP = 64
CHUNKS = 2


def split_pieces(x):
    high = x.astype(jnp.bfloat16)
    low = (x - high.astype(jnp.float32)).astype(jnp.bfloat16)
    return high, low


def pick_kernel(offset, table_ref, index_ref, extent_ref, tally_ref, out_ref):
    fields_count = out_ref.shape[1]
    slots = index_ref.shape[1]
    table_rows = table_ref.shape[0]
    columns = table_ref.shape[1]
    rows = table_rows // fields_count
    table = jnp.concatenate(split_pieces(table_ref[...]), axis=1)
    column_ids = lax.broadcasted_iota(jnp.int32, (columns, slots), 0)
    row_ids = lax.broadcasted_iota(jnp.int32, (8, slots), 0)
    slot_ids = lax.broadcasted_iota(jnp.int32, (1, slots), 1) + offset
    for owner in range(index_ref.shape[0]):
        index = index_ref[pl.ds(owner, 1), :]
        hot = (column_ids == index % columns).astype(jnp.bfloat16)
        by_column = jnp.dot(
            table, jnp.concatenate([hot, hot], axis=0), preferred_element_type=jnp.float32
        )
        row = index // columns
        masks = [row_ids + 8 * tile == row for tile in range(rows // 8)]
        weight = jnp.where(
            slot_ids < tally_ref[pl.ds(owner, 1), :], extent_ref[pl.ds(owner, 1), :], 0.0
        )
        for field in range(fields_count):
            chosen = jnp.zeros((8, slots), jnp.float32)
            for tile in range(rows // 8):
                start = field * rows + tile * 8
                chosen = jnp.where(masks[tile], by_column[start : start + 8], chosen)
            picked = jnp.sum(chosen, axis=0, keepdims=True)
            out_ref[owner, pl.ds(field, 1), :] = picked * weight


def pick_cells(surface_grid, indices, extent, tally, chunk, slots):
    fields_count, rows, columns = surface_grid.shape
    owners = indices.shape[0]
    table = surface_grid.reshape(fields_count * rows, columns)
    return pl.pallas_call(
        functools.partial(pick_kernel, chunk * slots),
        out_shape=jax.ShapeDtypeStruct((owners, fields_count, slots), jnp.float32),
        grid=(owners // GROUP,),
        in_specs=[
            pl.BlockSpec((fields_count * rows, columns), lambda i: (0, 0)),
            pl.BlockSpec((GROUP, slots), lambda i: (i, chunk)),
            pl.BlockSpec((GROUP, slots), lambda i: (i, chunk)),
            pl.BlockSpec((GROUP, 1), lambda i: (i, 0)),
        ],
        out_specs=pl.BlockSpec((GROUP, fields_count, slots), lambda i: (i, 0, 0)),
    )(table, indices, extent, tally[:, None])


def spread_kernel(has_start, final, value_ref, target_ref, *refs):
    if has_start:
        start_ref, refs = refs[0], refs[1:]
    out_ref = refs[0]
    acc_ref = refs[1] if final else out_ref
    fields_count = value_ref.shape[1]
    slots = value_ref.shape[2]
    lows = acc_ref.shape[1]
    highs = acc_ref.shape[0] // (2 * fields_count)

    @pl.when(pl.program_id(0) == 0)
    def _():
        if has_start:
            acc_ref[...] = start_ref[...]
        else:
            acc_ref[...] = jnp.zeros_like(acc_ref)

    high_ids = lax.broadcasted_iota(jnp.int32, (highs, slots), 0)
    low_ids = lax.broadcasted_iota(jnp.int32, (lows, slots), 0)
    total = jnp.zeros(acc_ref.shape, jnp.float32)
    for sender in range(target_ref.shape[0]):
        target = target_ref[pl.ds(sender, 1), :]
        high_hot = high_ids == target // lows
        low_hot = (low_ids == target % lows).astype(jnp.bfloat16)
        pieces = [part.astype(jnp.float32) for part in split_pieces(value_ref[sender])]
        weighted = jnp.concatenate(
            [
                jnp.where(high_hot, part[field : field + 1], 0.0).astype(jnp.bfloat16)
                for part in pieces
                for field in range(fields_count)
            ],
            axis=0,
        )
        total = total + lax.dot_general(
            weighted, low_hot, (((1,), (1,)), ((), ())), preferred_element_type=jnp.float32
        )
    acc_ref[...] += total

    if final:

        @pl.when(pl.program_id(0) == pl.num_programs(0) - 1)
        def _():
            half = fields_count * highs
            for field in range(fields_count):
                for high in range(highs):
                    row = field * highs + high
                    out_ref[pl.ds(field, 1), pl.ds(high * lows, lows)] = (
                        acc_ref[pl.ds(row, 1), :] + acc_ref[pl.ds(half + row, 1), :]
                    )


SPREAD_LOWS = 128


def spread_cells(values, targets, chunk, start, final):
    senders, fields_count, slots = values.shape
    highs = ACELL // SPREAD_LOWS
    shape = (2 * fields_count * highs, SPREAD_LOWS)
    in_specs = [
        pl.BlockSpec((GROUP, fields_count, slots), lambda i: (i, 0, 0)),
        pl.BlockSpec((GROUP, slots), lambda i: (i, chunk)),
    ]
    operands = [values, targets]
    if start is not None:
        in_specs.append(pl.BlockSpec(shape, lambda i: (0, 0)))
        operands.append(start)
    out_shape = (fields_count, ACELL) if final else shape
    return pl.pallas_call(
        functools.partial(spread_kernel, start is not None, final),
        out_shape=jax.ShapeDtypeStruct(out_shape, jnp.float32),
        grid=(senders // GROUP,),
        in_specs=in_specs,
        out_specs=pl.BlockSpec(out_shape, lambda i: (0, 0)),
        scratch_shapes=[pltpu.VMEM(shape, jnp.float32)] if final else [],
    )(*operands)


def local(
    starting_sea_elevation,
    zonal_integrated_flux,
    meridional_integrated_flux,
    ocean_strata_total,
    thermal_anomaly,
    zonal_baroclinic_velocity,
    meridional_baroclinic_velocity,
    sent_sender_mesh_index,
    sent_intersection_extent,
    sent_entry_tally,
    received_atmosphere_mesh_index,
):
    band_rows, band_columns = starting_sea_elevation.shape
    grid_rows = band_rows * lax.axis_size("lat")
    band = lax.axis_index("lat")
    depth = ocean_strata_total.astype(jnp.float32)
    planes = jnp.concatenate(
        [
            jnp.stack([starting_sea_elevation, zonal_integrated_flux, meridional_integrated_flux, depth]),
            thermal_anomaly,
        ],
        axis=0,
    )
    signs = jnp.array([1.0, -1.0, -1.0] + [1.0] * (1 + VERTICAL_STRATA), jnp.float32)
    ext = exchange(planes, signs, HALO)
    depth_ext = ext[3]
    wet = (depth_ext > 0).astype(jnp.float32)
    hnorm = depth_ext / VERTICAL_STRATA
    height = ext[0] * wet
    east = ext[1] * wet
    north = ext[2] * wet
    global_rows = band * band_rows - HALO + jnp.arange(band_rows + 2 * HALO)
    global_rows = jnp.where(global_rows >= grid_rows, 2 * grid_rows - 1 - global_rows, global_rows)
    rows = global_rows.astype(jnp.float32)
    rotation = (-spin_coef * jnp.cos(jnp.pi * (rows + 0.5) / grid_rows))[:, None]
    for step in range(STEPS):
        height = wet * (height - mass_coef * (east_of(east) - west_of(east) + (north_of(north) - south_of(north))))
        east = wet * (east - slope_coef * hnorm * (east_of(height) - west_of(height)) + rotation * north)
        north = wet * (north - slope_coef * hnorm * (north_of(height) - south_of(height)) - rotation * east)
    inner = (slice(HALO, HALO + band_rows), slice(HALO, HALO + band_columns))
    height = height[inner]
    east = east[inner]
    north = north[inner]
    near = (slice(None), slice(HALO - 1, HALO + band_rows + 1), slice(HALO - 1, HALO + band_columns + 1))
    levels_float = jnp.arange(VERTICAL_STRATA).astype(jnp.float32)[:, None, None]
    wet_wide = (levels_float < depth_ext[None][near]).astype(jnp.float32)
    tracer_wide = ext[4:][near] * wet_wide
    centre = (slice(None), slice(1, -1), slice(1, -1))
    submerged_stratum_mask = wet_wide[centre]
    passive_scalar_values = tracer_wide[centre]
    tracer_e = east_of(tracer_wide)[centre]
    tracer_w = west_of(tracer_wide)[centre]
    tracer_n = north_of(tracer_wide)[centre]
    tracer_s = south_of(tracer_wide)[centre]
    wet_e = east_of(wet_wide)[centre]
    wet_w = west_of(wet_wide)[centre]
    wet_n = north_of(wet_wide)[centre]
    wet_s = south_of(wet_wide)[centre]
    mixing = (
        wet_e * (tracer_e - passive_scalar_values)
        + wet_w * (tracer_w - passive_scalar_values)
        + wet_n * (tracer_n - passive_scalar_values)
        + wet_s * (tracer_s - passive_scalar_values)
    )
    speed_east = east[None] + zonal_baroclinic_velocity
    speed_north = north[None] + meridional_baroclinic_velocity
    carried = speed_east * (tracer_e - tracer_w) + speed_north * (tracer_n - tracer_s)
    tracer_new = submerged_stratum_mask * (
        passive_scalar_values + mix_coef * mixing - carry_coef * carried
    )
    surface_grid = jnp.stack([height, speed_east[0], speed_north[0], tracer_new[0]])
    slots = sent_sender_mesh_index.shape[2]
    width = slots // CHUNKS
    summed = None
    for chunk in range(CHUNKS):
        values = pick_cells(
            surface_grid,
            sent_sender_mesh_index[0],
            sent_intersection_extent[0],
            sent_entry_tally[0],
            chunk,
            width,
        )
        block = lax.all_to_all(values, ("lat", "lon"), split_axis=0, concat_axis=0, tiled=True)
        summed = spread_cells(
            block, received_atmosphere_mesh_index[0], chunk, summed, chunk == CHUNKS - 1
        )
    atmosphere = summed
    return (height, east, north, tracer_new, atmosphere)


def solution(mesh):
    in_specs = (
        P("lat", "lon"),
        P("lat", "lon"),
        P("lat", "lon"),
        P("lat", "lon"),
        P(None, "lat", "lon"),
        P(None, "lat", "lon"),
        P(None, "lat", "lon"),
        P(("lat", "lon"), None, None),
        P(("lat", "lon"), None, None),
        P(("lat", "lon"), None),
        P(("lat", "lon"), None, None),
    )
    out_specs = (
        P("lat", "lon"),
        P("lat", "lon"),
        P("lat", "lon"),
        P(None, "lat", "lon"),
        P(None, ("lat", "lon")),
    )
    return jax.shard_map(local, mesh=mesh, in_specs=in_specs, out_specs=out_specs, check_vma=False)
```

```python
import functools
import math

import jax
import jax.numpy as jnp
from jax import lax
from jax.experimental import pallas as pl
from jax.experimental.pallas import tpu as pltpu
from jax.sharding import PartitionSpec as P

VERTICAL_STRATA = 8
STEPS = 4
NF = 4
ACELL = 4096


mass_coef = 0.7
slope_coef = 0.7
spin_coef = 0.3
mix_coef = 0.1
carry_coef = 0.1


HALO = 2 * STEPS


def exchange(block, signs, width):
    planes, rows, columns = block.shape
    sectors = lax.axis_size("lon")
    bands = lax.axis_size("lat")
    eastward = [(i, (i + 1) % sectors) for i in range(sectors)]
    westward = [((i + 1) % sectors, i) for i in range(sectors)]
    from_west = lax.ppermute(block[:, :, columns - width :], "lon", eastward)
    from_east = lax.ppermute(block[:, :, :width], "lon", westward)
    wide = jnp.concatenate([from_west, block, from_east], axis=2)
    upward = [(b, b + 1) for b in range(bands - 1)]
    downward = [(b + 1, b) for b in range(bands - 1)]
    top = wide[:, rows - width :, :]
    from_south = lax.ppermute(top, "lat", upward)
    from_north = lax.ppermute(wide[:, :width, :], "lat", downward)
    last = (bands - 1) * sectors
    mirror = [(last + j, last + sectors - 1 - j) for j in range(sectors)]
    folded = lax.ppermute(top, ("lat", "lon"), mirror)
    folded = jnp.flip(folded, axis=(1, 2)) * signs[:, None, None]
    on_top = lax.axis_index("lat") == bands - 1
    north_rim = jnp.where(on_top, folded, from_north)
    return jnp.concatenate([from_south, wide, north_rim], axis=1)


def east_of(x):
    return jnp.concatenate([x[..., 1:], x[..., -1:]], axis=-1)


def west_of(x):
    return jnp.concatenate([x[..., :1], x[..., :-1]], axis=-1)


def north_of(x):
    return jnp.concatenate([x[..., 1:, :], x[..., -1:, :]], axis=-2)


def south_of(x):
    return jnp.concatenate([x[..., :1, :], x[..., :-1, :]], axis=-2)


GROUP = 64
SPREAD_GROUP = 128
CHUNKS = 2


def split_pieces(x):
    high = x.astype(jnp.bfloat16)
    low = (x - high.astype(jnp.float32)).astype(jnp.bfloat16)
    return high, low


def pick_kernel(offset, table_ref, index_ref, extent_ref, tally_ref, out_ref):
    fields_count = out_ref.shape[1]
    slots = index_ref.shape[1]
    table_rows = table_ref.shape[0]
    columns = table_ref.shape[1]
    rows = table_rows // fields_count
    table = jnp.concatenate(split_pieces(table_ref[...]), axis=1)
    column_ids = lax.broadcasted_iota(jnp.int32, (columns, slots), 0)
    row_ids = lax.broadcasted_iota(jnp.int32, (8, slots), 0)
    slot_ids = lax.broadcasted_iota(jnp.int32, (1, slots), 1) + offset
    for owner in range(index_ref.shape[0]):
        index = index_ref[pl.ds(owner, 1), :]
        hot = (column_ids == index % columns).astype(jnp.bfloat16)
        by_column = jnp.dot(
            table, jnp.concatenate([hot, hot], axis=0), preferred_element_type=jnp.float32
        )
        row = index // columns
        masks = [row_ids + 8 * tile == row for tile in range(rows // 8)]
        weight = jnp.where(
            slot_ids < tally_ref[pl.ds(owner, 1), :], extent_ref[pl.ds(owner, 1), :], 0.0
        )
        for field in range(fields_count):
            chosen = jnp.zeros((8, slots), jnp.float32)
            for tile in range(rows // 8):
                start = field * rows + tile * 8
                chosen = jnp.where(masks[tile], by_column[start : start + 8], chosen)
            picked = jnp.sum(chosen, axis=0, keepdims=True)
            out_ref[owner, pl.ds(field, 1), :] = picked * weight


def pick_cells(surface_grid, indices, extent, tally, chunk, slots):
    fields_count, rows, columns = surface_grid.shape
    owners = indices.shape[0]
    table = surface_grid.reshape(fields_count * rows, columns)
    return pl.pallas_call(
        functools.partial(pick_kernel, chunk * slots),
        out_shape=jax.ShapeDtypeStruct((owners, fields_count, slots), jnp.float32),
        grid=(owners // GROUP,),
        in_specs=[
            pl.BlockSpec((fields_count * rows, columns), lambda i: (0, 0)),
            pl.BlockSpec((GROUP, slots), lambda i: (i, chunk)),
            pl.BlockSpec((GROUP, slots), lambda i: (i, chunk)),
            pl.BlockSpec((GROUP, 1), lambda i: (i, 0)),
        ],
        out_specs=pl.BlockSpec((GROUP, fields_count, slots), lambda i: (i, 0, 0)),
    )(table, indices, extent, tally[:, None])


def spread_kernel(has_start, final, value_ref, target_ref, *refs):
    if has_start:
        start_ref, refs = refs[0], refs[1:]
    out_ref = refs[0]
    acc_ref = refs[1] if final else out_ref
    fields_count = value_ref.shape[1]
    slots = value_ref.shape[2]
    lows = acc_ref.shape[1]
    highs = acc_ref.shape[0] // (2 * fields_count)

    @pl.when(pl.program_id(0) == 0)
    def _():
        if has_start:
            acc_ref[...] = start_ref[...]
        else:
            acc_ref[...] = jnp.zeros_like(acc_ref)

    high_ids = lax.broadcasted_iota(jnp.int32, (highs, slots), 0)
    low_ids = lax.broadcasted_iota(jnp.int32, (lows, slots), 0)
    total = jnp.zeros(acc_ref.shape, jnp.float32)
    for sender in range(target_ref.shape[0]):
        target = target_ref[pl.ds(sender, 1), :]
        high_hot = high_ids == target // lows
        low_hot = (low_ids == target % lows).astype(jnp.bfloat16)
        pieces = [part.astype(jnp.float32) for part in split_pieces(value_ref[sender])]
        weighted = jnp.concatenate(
            [
                jnp.where(high_hot, part[field : field + 1], 0.0).astype(jnp.bfloat16)
                for part in pieces
                for field in range(fields_count)
            ],
            axis=0,
        )
        total = total + lax.dot_general(
            weighted, low_hot, (((1,), (1,)), ((), ())), preferred_element_type=jnp.float32
        )
    acc_ref[...] += total

    if final:

        @pl.when(pl.program_id(0) == pl.num_programs(0) - 1)
        def _():
            half = fields_count * highs
            for field in range(fields_count):
                for high in range(highs):
                    row = field * highs + high
                    out_ref[pl.ds(field, 1), pl.ds(high * lows, lows)] = (
                        acc_ref[pl.ds(row, 1), :] + acc_ref[pl.ds(half + row, 1), :]
                    )


SPREAD_LOWS = 128


def spread_cells(values, targets, chunk, start, final):
    senders, fields_count, slots = values.shape
    highs = ACELL // SPREAD_LOWS
    shape = (2 * fields_count * highs, SPREAD_LOWS)
    in_specs = [
        pl.BlockSpec((SPREAD_GROUP, fields_count, slots), lambda i: (i, 0, 0)),
        pl.BlockSpec((SPREAD_GROUP, slots), lambda i: (i, chunk)),
    ]
    operands = [values, targets]
    if start is not None:
        in_specs.append(pl.BlockSpec(shape, lambda i: (0, 0)))
        operands.append(start)
    out_shape = (fields_count, ACELL) if final else shape
    return pl.pallas_call(
        functools.partial(spread_kernel, start is not None, final),
        out_shape=jax.ShapeDtypeStruct(out_shape, jnp.float32),
        grid=(senders // SPREAD_GROUP,),
        in_specs=in_specs,
        out_specs=pl.BlockSpec(out_shape, lambda i: (0, 0)),
        scratch_shapes=[pltpu.VMEM(shape, jnp.float32)] if final else [],
    )(*operands)


def local(
    starting_sea_elevation,
    zonal_integrated_flux,
    meridional_integrated_flux,
    ocean_strata_total,
    thermal_anomaly,
    zonal_baroclinic_velocity,
    meridional_baroclinic_velocity,
    sent_sender_mesh_index,
    sent_intersection_extent,
    sent_entry_tally,
    received_atmosphere_mesh_index,
):
    band_rows, band_columns = starting_sea_elevation.shape
    grid_rows = band_rows * lax.axis_size("lat")
    band = lax.axis_index("lat")
    depth = ocean_strata_total.astype(jnp.float32)
    planes = jnp.concatenate(
        [
            jnp.stack([starting_sea_elevation, zonal_integrated_flux, meridional_integrated_flux, depth]),
            thermal_anomaly,
        ],
        axis=0,
    )
    signs = jnp.array([1.0, -1.0, -1.0] + [1.0] * (1 + VERTICAL_STRATA), jnp.float32)
    ext = exchange(planes, signs, HALO)
    depth_ext = ext[3]
    wet = (depth_ext > 0).astype(jnp.float32)
    hnorm = depth_ext / VERTICAL_STRATA
    height = ext[0] * wet
    east = ext[1] * wet
    north = ext[2] * wet
    global_rows = band * band_rows - HALO + jnp.arange(band_rows + 2 * HALO)
    global_rows = jnp.where(global_rows >= grid_rows, 2 * grid_rows - 1 - global_rows, global_rows)
    rows = global_rows.astype(jnp.float32)
    rotation = (-spin_coef * jnp.cos(jnp.pi * (rows + 0.5) / grid_rows))[:, None]
    for step in range(STEPS):
        height = wet * (height - mass_coef * (east_of(east) - west_of(east) + (north_of(north) - south_of(north))))
        east = wet * (east - slope_coef * hnorm * (east_of(height) - west_of(height)) + rotation * north)
        north = wet * (north - slope_coef * hnorm * (north_of(height) - south_of(height)) - rotation * east)
    inner = (slice(HALO, HALO + band_rows), slice(HALO, HALO + band_columns))
    height = height[inner]
    east = east[inner]
    north = north[inner]
    near = (slice(None), slice(HALO - 1, HALO + band_rows + 1), slice(HALO - 1, HALO + band_columns + 1))
    levels_float = jnp.arange(VERTICAL_STRATA).astype(jnp.float32)[:, None, None]
    wet_wide = (levels_float < depth_ext[None][near]).astype(jnp.float32)
    tracer_wide = ext[4:][near] * wet_wide
    centre = (slice(None), slice(1, -1), slice(1, -1))
    submerged_stratum_mask = wet_wide[centre]
    passive_scalar_values = tracer_wide[centre]
    tracer_e = east_of(tracer_wide)[centre]
    tracer_w = west_of(tracer_wide)[centre]
    tracer_n = north_of(tracer_wide)[centre]
    tracer_s = south_of(tracer_wide)[centre]
    wet_e = east_of(wet_wide)[centre]
    wet_w = west_of(wet_wide)[centre]
    wet_n = north_of(wet_wide)[centre]
    wet_s = south_of(wet_wide)[centre]
    mixing = (
        wet_e * (tracer_e - passive_scalar_values)
        + wet_w * (tracer_w - passive_scalar_values)
        + wet_n * (tracer_n - passive_scalar_values)
        + wet_s * (tracer_s - passive_scalar_values)
    )
    speed_east = east[None] + zonal_baroclinic_velocity
    speed_north = north[None] + meridional_baroclinic_velocity
    carried = speed_east * (tracer_e - tracer_w) + speed_north * (tracer_n - tracer_s)
    tracer_new = submerged_stratum_mask * (
        passive_scalar_values + mix_coef * mixing - carry_coef * carried
    )
    surface_grid = jnp.stack([height, speed_east[0], speed_north[0], tracer_new[0]])
    slots = sent_sender_mesh_index.shape[2]
    width = slots // CHUNKS
    summed = None
    for chunk in range(CHUNKS):
        values = pick_cells(
            surface_grid,
            sent_sender_mesh_index[0],
            sent_intersection_extent[0],
            sent_entry_tally[0],
            chunk,
            width,
        )
        block = lax.all_to_all(values, ("lat", "lon"), split_axis=0, concat_axis=0, tiled=True)
        summed = spread_cells(
            block, received_atmosphere_mesh_index[0], chunk, summed, chunk == CHUNKS - 1
        )
    atmosphere = summed
    return (height, east, north, tracer_new, atmosphere)


def solution(mesh):
    in_specs = (
        P("lat", "lon"),
        P("lat", "lon"),
        P("lat", "lon"),
        P("lat", "lon"),
        P(None, "lat", "lon"),
        P(None, "lat", "lon"),
        P(None, "lat", "lon"),
        P(("lat", "lon"), None, None),
        P(("lat", "lon"), None, None),
        P(("lat", "lon"), None),
        P(("lat", "lon"), None, None),
    )
    out_specs = (
        P("lat", "lon"),
        P("lat", "lon"),
        P("lat", "lon"),
        P(None, "lat", "lon"),
        P(None, ("lat", "lon")),
    )
    return jax.shard_map(local, mesh=mesh, in_specs=in_specs, out_specs=out_specs, check_vma=False)
```

```python
import functools
import math

import jax
import jax.numpy as jnp
from jax import lax
from jax.experimental import pallas as pl
from jax.experimental.pallas import tpu as pltpu
from jax.sharding import PartitionSpec as P

VERTICAL_STRATA = 8
STEPS = 4
NF = 4
ACELL = 4096


mass_coef = 0.7
slope_coef = 0.7
spin_coef = 0.3
mix_coef = 0.1
carry_coef = 0.1


HALO = 2 * STEPS


def exchange(block, signs, width):
    planes, rows, columns = block.shape
    sectors = lax.axis_size("lon")
    bands = lax.axis_size("lat")
    eastward = [(i, (i + 1) % sectors) for i in range(sectors)]
    westward = [((i + 1) % sectors, i) for i in range(sectors)]
    from_west = lax.ppermute(block[:, :, columns - width :], "lon", eastward)
    from_east = lax.ppermute(block[:, :, :width], "lon", westward)
    wide = jnp.concatenate([from_west, block, from_east], axis=2)
    upward = [(b, b + 1) for b in range(bands - 1)]
    downward = [(b + 1, b) for b in range(bands - 1)]
    top = wide[:, rows - width :, :]
    from_south = lax.ppermute(top, "lat", upward)
    from_north = lax.ppermute(wide[:, :width, :], "lat", downward)
    last = (bands - 1) * sectors
    mirror = [(last + j, last + sectors - 1 - j) for j in range(sectors)]
    folded = lax.ppermute(top, ("lat", "lon"), mirror)
    folded = jnp.flip(folded, axis=(1, 2)) * signs[:, None, None]
    on_top = lax.axis_index("lat") == bands - 1
    north_rim = jnp.where(on_top, folded, from_north)
    return jnp.concatenate([from_south, wide, north_rim], axis=1)


def east_of(x):
    return jnp.concatenate([x[..., 1:], x[..., -1:]], axis=-1)


def west_of(x):
    return jnp.concatenate([x[..., :1], x[..., :-1]], axis=-1)


def north_of(x):
    return jnp.concatenate([x[..., 1:, :], x[..., -1:, :]], axis=-2)


def south_of(x):
    return jnp.concatenate([x[..., :1, :], x[..., :-1, :]], axis=-2)


GROUP = 64
CHUNKS = 2


def split_pieces(x):
    high = x.astype(jnp.bfloat16)
    low = (x - high.astype(jnp.float32)).astype(jnp.bfloat16)
    return high, low


def pick_kernel(offset, table_ref, index_ref, extent_ref, tally_ref, out_ref):
    fields_count = out_ref.shape[1]
    slots = index_ref.shape[1]
    table_rows = table_ref.shape[0]
    columns = table_ref.shape[1]
    rows = table_rows // fields_count
    table = jnp.concatenate(split_pieces(table_ref[...]), axis=1)
    column_ids = lax.broadcasted_iota(jnp.int32, (columns, slots), 0)
    row_ids = lax.broadcasted_iota(jnp.int32, (8, slots), 0)
    owners = index_ref.shape[0]
    slot_ids = lax.broadcasted_iota(jnp.int32, (owners, slots), 1) + offset
    indices = index_ref[...]
    column_all = indices % columns
    row_all = indices // columns
    weight_all = jnp.where(slot_ids < tally_ref[...], extent_ref[...], 0.0)
    for owner in range(owners):
        hot = (column_ids == column_all[owner : owner + 1]).astype(jnp.bfloat16)
        by_column = jnp.dot(
            table, jnp.concatenate([hot, hot], axis=0), preferred_element_type=jnp.float32
        )
        row = row_all[owner : owner + 1]
        masks = [row_ids + 8 * tile == row for tile in range(rows // 8)]
        weight = weight_all[owner : owner + 1]
        for field in range(fields_count):
            chosen = jnp.zeros((8, slots), jnp.float32)
            for tile in range(rows // 8):
                start = field * rows + tile * 8
                chosen = jnp.where(masks[tile], by_column[start : start + 8], chosen)
            picked = jnp.sum(chosen, axis=0, keepdims=True)
            out_ref[owner, pl.ds(field, 1), :] = picked * weight


def pick_cells(surface_grid, indices, extent, tally, chunk, slots):
    fields_count, rows, columns = surface_grid.shape
    owners = indices.shape[0]
    table = surface_grid.reshape(fields_count * rows, columns)
    return pl.pallas_call(
        functools.partial(pick_kernel, chunk * slots),
        out_shape=jax.ShapeDtypeStruct((owners, fields_count, slots), jnp.float32),
        grid=(owners // GROUP,),
        in_specs=[
            pl.BlockSpec((fields_count * rows, columns), lambda i: (0, 0)),
            pl.BlockSpec((GROUP, slots), lambda i: (i, chunk)),
            pl.BlockSpec((GROUP, slots), lambda i: (i, chunk)),
            pl.BlockSpec((GROUP, 1), lambda i: (i, 0)),
        ],
        out_specs=pl.BlockSpec((GROUP, fields_count, slots), lambda i: (i, 0, 0)),
    )(table, indices, extent, tally[:, None])


def spread_kernel(has_start, final, value_ref, target_ref, *refs):
    if has_start:
        start_ref, refs = refs[0], refs[1:]
    out_ref = refs[0]
    acc_ref = refs[1] if final else out_ref
    fields_count = value_ref.shape[1]
    slots = value_ref.shape[2]
    lows = acc_ref.shape[1]
    highs = acc_ref.shape[0] // (2 * fields_count)

    @pl.when(pl.program_id(0) == 0)
    def _():
        if has_start:
            acc_ref[...] = start_ref[...]
        else:
            acc_ref[...] = jnp.zeros_like(acc_ref)

    high_ids = lax.broadcasted_iota(jnp.int32, (highs, slots), 0)
    low_ids = lax.broadcasted_iota(jnp.int32, (lows, slots), 0)
    total = jnp.zeros(acc_ref.shape, jnp.float32)
    for sender in range(target_ref.shape[0]):
        target = target_ref[pl.ds(sender, 1), :]
        high_hot = high_ids == target // lows
        low_hot = (low_ids == target % lows).astype(jnp.bfloat16)
        pieces = [part.astype(jnp.float32) for part in split_pieces(value_ref[sender])]
        weighted = jnp.concatenate(
            [
                jnp.where(high_hot, part[field : field + 1], 0.0).astype(jnp.bfloat16)
                for part in pieces
                for field in range(fields_count)
            ],
            axis=0,
        )
        total = total + lax.dot_general(
            weighted, low_hot, (((1,), (1,)), ((), ())), preferred_element_type=jnp.float32
        )
    acc_ref[...] += total

    if final:

        @pl.when(pl.program_id(0) == pl.num_programs(0) - 1)
        def _():
            half = fields_count * highs
            for field in range(fields_count):
                for high in range(highs):
                    row = field * highs + high
                    out_ref[pl.ds(field, 1), pl.ds(high * lows, lows)] = (
                        acc_ref[pl.ds(row, 1), :] + acc_ref[pl.ds(half + row, 1), :]
                    )


SPREAD_LOWS = 128


def spread_cells(values, targets, chunk, start, final):
    senders, fields_count, slots = values.shape
    highs = ACELL // SPREAD_LOWS
    shape = (2 * fields_count * highs, SPREAD_LOWS)
    in_specs = [
        pl.BlockSpec((GROUP, fields_count, slots), lambda i: (i, 0, 0)),
        pl.BlockSpec((GROUP, slots), lambda i: (i, chunk)),
    ]
    operands = [values, targets]
    if start is not None:
        in_specs.append(pl.BlockSpec(shape, lambda i: (0, 0)))
        operands.append(start)
    out_shape = (fields_count, ACELL) if final else shape
    return pl.pallas_call(
        functools.partial(spread_kernel, start is not None, final),
        out_shape=jax.ShapeDtypeStruct(out_shape, jnp.float32),
        grid=(senders // GROUP,),
        in_specs=in_specs,
        out_specs=pl.BlockSpec(out_shape, lambda i: (0, 0)),
        scratch_shapes=[pltpu.VMEM(shape, jnp.float32)] if final else [],
    )(*operands)


def local(
    starting_sea_elevation,
    zonal_integrated_flux,
    meridional_integrated_flux,
    ocean_strata_total,
    thermal_anomaly,
    zonal_baroclinic_velocity,
    meridional_baroclinic_velocity,
    sent_sender_mesh_index,
    sent_intersection_extent,
    sent_entry_tally,
    received_atmosphere_mesh_index,
):
    band_rows, band_columns = starting_sea_elevation.shape
    grid_rows = band_rows * lax.axis_size("lat")
    band = lax.axis_index("lat")
    depth = ocean_strata_total.astype(jnp.float32)
    planes = jnp.concatenate(
        [
            jnp.stack([starting_sea_elevation, zonal_integrated_flux, meridional_integrated_flux, depth]),
            thermal_anomaly,
        ],
        axis=0,
    )
    signs = jnp.array([1.0, -1.0, -1.0] + [1.0] * (1 + VERTICAL_STRATA), jnp.float32)
    ext = exchange(planes, signs, HALO)
    depth_ext = ext[3]
    wet = (depth_ext > 0).astype(jnp.float32)
    hnorm = depth_ext / VERTICAL_STRATA
    height = ext[0] * wet
    east = ext[1] * wet
    north = ext[2] * wet
    global_rows = band * band_rows - HALO + jnp.arange(band_rows + 2 * HALO)
    global_rows = jnp.where(global_rows >= grid_rows, 2 * grid_rows - 1 - global_rows, global_rows)
    rows = global_rows.astype(jnp.float32)
    rotation = (-spin_coef * jnp.cos(jnp.pi * (rows + 0.5) / grid_rows))[:, None]
    for step in range(STEPS):
        height = wet * (height - mass_coef * (east_of(east) - west_of(east) + (north_of(north) - south_of(north))))
        east = wet * (east - slope_coef * hnorm * (east_of(height) - west_of(height)) + rotation * north)
        north = wet * (north - slope_coef * hnorm * (north_of(height) - south_of(height)) - rotation * east)
    inner = (slice(HALO, HALO + band_rows), slice(HALO, HALO + band_columns))
    height = height[inner]
    east = east[inner]
    north = north[inner]
    near = (slice(None), slice(HALO - 1, HALO + band_rows + 1), slice(HALO - 1, HALO + band_columns + 1))
    levels_float = jnp.arange(VERTICAL_STRATA).astype(jnp.float32)[:, None, None]
    wet_wide = (levels_float < depth_ext[None][near]).astype(jnp.float32)
    tracer_wide = ext[4:][near] * wet_wide
    centre = (slice(None), slice(1, -1), slice(1, -1))
    submerged_stratum_mask = wet_wide[centre]
    passive_scalar_values = tracer_wide[centre]
    tracer_e = east_of(tracer_wide)[centre]
    tracer_w = west_of(tracer_wide)[centre]
    tracer_n = north_of(tracer_wide)[centre]
    tracer_s = south_of(tracer_wide)[centre]
    wet_e = east_of(wet_wide)[centre]
    wet_w = west_of(wet_wide)[centre]
    wet_n = north_of(wet_wide)[centre]
    wet_s = south_of(wet_wide)[centre]
    mixing = (
        wet_e * (tracer_e - passive_scalar_values)
        + wet_w * (tracer_w - passive_scalar_values)
        + wet_n * (tracer_n - passive_scalar_values)
        + wet_s * (tracer_s - passive_scalar_values)
    )
    speed_east = east[None] + zonal_baroclinic_velocity
    speed_north = north[None] + meridional_baroclinic_velocity
    carried = speed_east * (tracer_e - tracer_w) + speed_north * (tracer_n - tracer_s)
    tracer_new = submerged_stratum_mask * (
        passive_scalar_values + mix_coef * mixing - carry_coef * carried
    )
    surface_grid = jnp.stack([height, speed_east[0], speed_north[0], tracer_new[0]])
    slots = sent_sender_mesh_index.shape[2]
    width = slots // CHUNKS
    summed = None
    for chunk in range(CHUNKS):
        values = pick_cells(
            surface_grid,
            sent_sender_mesh_index[0],
            sent_intersection_extent[0],
            sent_entry_tally[0],
            chunk,
            width,
        )
        block = lax.all_to_all(values, ("lat", "lon"), split_axis=0, concat_axis=0, tiled=True)
        summed = spread_cells(
            block, received_atmosphere_mesh_index[0], chunk, summed, chunk == CHUNKS - 1
        )
    atmosphere = summed
    return (height, east, north, tracer_new, atmosphere)


def solution(mesh):
    in_specs = (
        P("lat", "lon"),
        P("lat", "lon"),
        P("lat", "lon"),
        P("lat", "lon"),
        P(None, "lat", "lon"),
        P(None, "lat", "lon"),
        P(None, "lat", "lon"),
        P(("lat", "lon"), None, None),
        P(("lat", "lon"), None, None),
        P(("lat", "lon"), None),
        P(("lat", "lon"), None, None),
    )
    out_specs = (
        P("lat", "lon"),
        P("lat", "lon"),
        P("lat", "lon"),
        P(None, "lat", "lon"),
        P(None, ("lat", "lon")),
    )
    return jax.shard_map(local, mesh=mesh, in_specs=in_specs, out_specs=out_specs, check_vma=False)
```

```python
import functools
import math

import jax
import jax.numpy as jnp
from jax import lax
from jax.experimental import pallas as pl
from jax.experimental.pallas import tpu as pltpu
from jax.sharding import PartitionSpec as P

VERTICAL_STRATA = 8
STEPS = 4
NF = 4
ACELL = 4096


mass_coef = 0.7
slope_coef = 0.7
spin_coef = 0.3
mix_coef = 0.1
carry_coef = 0.1


HALO = 2 * STEPS


def exchange(block, signs, width):
    planes, rows, columns = block.shape
    sectors = lax.axis_size("lon")
    bands = lax.axis_size("lat")
    eastward = [(i, (i + 1) % sectors) for i in range(sectors)]
    westward = [((i + 1) % sectors, i) for i in range(sectors)]
    from_west = lax.ppermute(block[:, :, columns - width :], "lon", eastward)
    from_east = lax.ppermute(block[:, :, :width], "lon", westward)
    wide = jnp.concatenate([from_west, block, from_east], axis=2)
    upward = [(b, b + 1) for b in range(bands - 1)]
    downward = [(b + 1, b) for b in range(bands - 1)]
    top = wide[:, rows - width :, :]
    from_south = lax.ppermute(top, "lat", upward)
    from_north = lax.ppermute(wide[:, :width, :], "lat", downward)
    last = (bands - 1) * sectors
    mirror = [(last + j, last + sectors - 1 - j) for j in range(sectors)]
    folded = lax.ppermute(top, ("lat", "lon"), mirror)
    folded = jnp.flip(folded, axis=(1, 2)) * signs[:, None, None]
    on_top = lax.axis_index("lat") == bands - 1
    north_rim = jnp.where(on_top, folded, from_north)
    return jnp.concatenate([from_south, wide, north_rim], axis=1)


def east_of(x):
    return jnp.concatenate([x[..., 1:], x[..., -1:]], axis=-1)


def west_of(x):
    return jnp.concatenate([x[..., :1], x[..., :-1]], axis=-1)


def north_of(x):
    return jnp.concatenate([x[..., 1:, :], x[..., -1:, :]], axis=-2)


def south_of(x):
    return jnp.concatenate([x[..., :1, :], x[..., :-1, :]], axis=-2)


GROUP = 64
CHUNKS = 2


def split_pieces(x):
    high = x.astype(jnp.bfloat16)
    low = (x - high.astype(jnp.float32)).astype(jnp.bfloat16)
    return high, low


def pick_kernel(offset, table_ref, index_ref, extent_ref, tally_ref, out_ref):
    fields_count = out_ref.shape[1]
    slots = index_ref.shape[1]
    table_rows = table_ref.shape[0]
    columns = table_ref.shape[1]
    rows = table_rows // fields_count
    table = jnp.concatenate(split_pieces(table_ref[...]), axis=1)
    column_ids = lax.broadcasted_iota(jnp.int32, (columns, slots), 0)
    row_ids = lax.broadcasted_iota(jnp.int32, (8, slots), 0)
    owners = index_ref.shape[0]
    slot_ids = lax.broadcasted_iota(jnp.int32, (owners, slots), 1) + offset
    indices = index_ref[...]
    column_all = indices % columns
    row_all = indices // columns
    weight_all = jnp.where(slot_ids < tally_ref[...], extent_ref[...], 0.0)
    for owner in range(owners):
        hot = (column_ids == column_all[owner : owner + 1]).astype(jnp.bfloat16)
        by_column = jnp.dot(
            table, jnp.concatenate([hot, hot], axis=0), preferred_element_type=jnp.float32
        )
        row = row_all[owner : owner + 1]
        masks = [row_ids + 8 * tile == row for tile in range(rows // 8)]
        weight = weight_all[owner : owner + 1]
        for field in range(fields_count):
            chosen = jnp.zeros((8, slots), jnp.float32)
            for tile in range(rows // 8):
                start = field * rows + tile * 8
                chosen = jnp.where(masks[tile], by_column[start : start + 8], chosen)
            picked = jnp.sum(chosen, axis=0, keepdims=True)
            out_ref[owner, pl.ds(field, 1), :] = picked * weight


def pick_cells(surface_grid, indices, extent, tally, chunk, slots):
    fields_count, rows, columns = surface_grid.shape
    owners = indices.shape[0]
    table = surface_grid.reshape(fields_count * rows, columns)
    return pl.pallas_call(
        functools.partial(pick_kernel, chunk * slots),
        out_shape=jax.ShapeDtypeStruct((owners, fields_count, slots), jnp.float32),
        grid=(owners // GROUP,),
        in_specs=[
            pl.BlockSpec((fields_count * rows, columns), lambda i: (0, 0)),
            pl.BlockSpec((GROUP, slots), lambda i: (i, chunk)),
            pl.BlockSpec((GROUP, slots), lambda i: (i, chunk)),
            pl.BlockSpec((GROUP, 1), lambda i: (i, 0)),
        ],
        out_specs=pl.BlockSpec((GROUP, fields_count, slots), lambda i: (i, 0, 0)),
    )(table, indices, extent, tally[:, None])


def spread_kernel(has_start, final, value_ref, target_ref, *refs):
    if has_start:
        start_ref, refs = refs[0], refs[1:]
    out_ref = refs[0]
    acc_ref = refs[1] if final else out_ref
    fields_count = value_ref.shape[1]
    slots = value_ref.shape[2]
    lows = acc_ref.shape[1]
    highs = acc_ref.shape[0] // (2 * fields_count)

    @pl.when(pl.program_id(0) == 0)
    def _():
        if has_start:
            acc_ref[...] = start_ref[...]
        else:
            acc_ref[...] = jnp.zeros_like(acc_ref)

    high_ids = lax.broadcasted_iota(jnp.int32, (highs, slots), 0)
    low_ids = lax.broadcasted_iota(jnp.int32, (lows, slots), 0)
    total = jnp.zeros(acc_ref.shape, jnp.float32)
    targets = target_ref[...]
    high_all = targets // lows
    low_all = targets % lows
    for sender in range(target_ref.shape[0]):
        high_hot = high_ids == high_all[sender : sender + 1]
        low_hot = (low_ids == low_all[sender : sender + 1]).astype(jnp.bfloat16)
        pieces = [part.astype(jnp.float32) for part in split_pieces(value_ref[sender])]
        weighted = jnp.concatenate(
            [
                jnp.where(high_hot, part[field : field + 1], 0.0).astype(jnp.bfloat16)
                for part in pieces
                for field in range(fields_count)
            ],
            axis=0,
        )
        total = total + lax.dot_general(
            weighted, low_hot, (((1,), (1,)), ((), ())), preferred_element_type=jnp.float32
        )
    acc_ref[...] += total

    if final:

        @pl.when(pl.program_id(0) == pl.num_programs(0) - 1)
        def _():
            half = fields_count * highs
            for field in range(fields_count):
                for high in range(highs):
                    row = field * highs + high
                    out_ref[pl.ds(field, 1), pl.ds(high * lows, lows)] = (
                        acc_ref[pl.ds(row, 1), :] + acc_ref[pl.ds(half + row, 1), :]
                    )


SPREAD_LOWS = 128


def spread_cells(values, targets, chunk, start, final):
    senders, fields_count, slots = values.shape
    highs = ACELL // SPREAD_LOWS
    shape = (2 * fields_count * highs, SPREAD_LOWS)
    in_specs = [
        pl.BlockSpec((GROUP, fields_count, slots), lambda i: (i, 0, 0)),
        pl.BlockSpec((GROUP, slots), lambda i: (i, chunk)),
    ]
    operands = [values, targets]
    if start is not None:
        in_specs.append(pl.BlockSpec(shape, lambda i: (0, 0)))
        operands.append(start)
    out_shape = (fields_count, ACELL) if final else shape
    return pl.pallas_call(
        functools.partial(spread_kernel, start is not None, final),
        out_shape=jax.ShapeDtypeStruct(out_shape, jnp.float32),
        grid=(senders // GROUP,),
        in_specs=in_specs,
        out_specs=pl.BlockSpec(out_shape, lambda i: (0, 0)),
        scratch_shapes=[pltpu.VMEM(shape, jnp.float32)] if final else [],
    )(*operands)


def local(
    starting_sea_elevation,
    zonal_integrated_flux,
    meridional_integrated_flux,
    ocean_strata_total,
    thermal_anomaly,
    zonal_baroclinic_velocity,
    meridional_baroclinic_velocity,
    sent_sender_mesh_index,
    sent_intersection_extent,
    sent_entry_tally,
    received_atmosphere_mesh_index,
):
    band_rows, band_columns = starting_sea_elevation.shape
    grid_rows = band_rows * lax.axis_size("lat")
    band = lax.axis_index("lat")
    depth = ocean_strata_total.astype(jnp.float32)
    planes = jnp.concatenate(
        [
            jnp.stack([starting_sea_elevation, zonal_integrated_flux, meridional_integrated_flux, depth]),
            thermal_anomaly,
        ],
        axis=0,
    )
    signs = jnp.array([1.0, -1.0, -1.0] + [1.0] * (1 + VERTICAL_STRATA), jnp.float32)
    ext = exchange(planes, signs, HALO)
    depth_ext = ext[3]
    wet = (depth_ext > 0).astype(jnp.float32)
    hnorm = depth_ext / VERTICAL_STRATA
    height = ext[0] * wet
    east = ext[1] * wet
    north = ext[2] * wet
    global_rows = band * band_rows - HALO + jnp.arange(band_rows + 2 * HALO)
    global_rows = jnp.where(global_rows >= grid_rows, 2 * grid_rows - 1 - global_rows, global_rows)
    rows = global_rows.astype(jnp.float32)
    rotation = (-spin_coef * jnp.cos(jnp.pi * (rows + 0.5) / grid_rows))[:, None]
    for step in range(STEPS):
        height = wet * (height - mass_coef * (east_of(east) - west_of(east) + (north_of(north) - south_of(north))))
        east = wet * (east - slope_coef * hnorm * (east_of(height) - west_of(height)) + rotation * north)
        north = wet * (north - slope_coef * hnorm * (north_of(height) - south_of(height)) - rotation * east)
    inner = (slice(HALO, HALO + band_rows), slice(HALO, HALO + band_columns))
    height = height[inner]
    east = east[inner]
    north = north[inner]
    near = (slice(None), slice(HALO - 1, HALO + band_rows + 1), slice(HALO - 1, HALO + band_columns + 1))
    levels_float = jnp.arange(VERTICAL_STRATA).astype(jnp.float32)[:, None, None]
    wet_wide = (levels_float < depth_ext[None][near]).astype(jnp.float32)
    tracer_wide = ext[4:][near] * wet_wide
    centre = (slice(None), slice(1, -1), slice(1, -1))
    submerged_stratum_mask = wet_wide[centre]
    passive_scalar_values = tracer_wide[centre]
    tracer_e = east_of(tracer_wide)[centre]
    tracer_w = west_of(tracer_wide)[centre]
    tracer_n = north_of(tracer_wide)[centre]
    tracer_s = south_of(tracer_wide)[centre]
    wet_e = east_of(wet_wide)[centre]
    wet_w = west_of(wet_wide)[centre]
    wet_n = north_of(wet_wide)[centre]
    wet_s = south_of(wet_wide)[centre]
    mixing = (
        wet_e * (tracer_e - passive_scalar_values)
        + wet_w * (tracer_w - passive_scalar_values)
        + wet_n * (tracer_n - passive_scalar_values)
        + wet_s * (tracer_s - passive_scalar_values)
    )
    speed_east = east[None] + zonal_baroclinic_velocity
    speed_north = north[None] + meridional_baroclinic_velocity
    carried = speed_east * (tracer_e - tracer_w) + speed_north * (tracer_n - tracer_s)
    tracer_new = submerged_stratum_mask * (
        passive_scalar_values + mix_coef * mixing - carry_coef * carried
    )
    surface_grid = jnp.stack([height, speed_east[0], speed_north[0], tracer_new[0]])
    slots = sent_sender_mesh_index.shape[2]
    width = slots // CHUNKS
    summed = None
    for chunk in range(CHUNKS):
        values = pick_cells(
            surface_grid,
            sent_sender_mesh_index[0],
            sent_intersection_extent[0],
            sent_entry_tally[0],
            chunk,
            width,
        )
        block = lax.all_to_all(values, ("lat", "lon"), split_axis=0, concat_axis=0, tiled=True)
        summed = spread_cells(
            block, received_atmosphere_mesh_index[0], chunk, summed, chunk == CHUNKS - 1
        )
    atmosphere = summed
    return (height, east, north, tracer_new, atmosphere)


def solution(mesh):
    in_specs = (
        P("lat", "lon"),
        P("lat", "lon"),
        P("lat", "lon"),
        P("lat", "lon"),
        P(None, "lat", "lon"),
        P(None, "lat", "lon"),
        P(None, "lat", "lon"),
        P(("lat", "lon"), None, None),
        P(("lat", "lon"), None, None),
        P(("lat", "lon"), None),
        P(("lat", "lon"), None, None),
    )
    out_specs = (
        P("lat", "lon"),
        P("lat", "lon"),
        P("lat", "lon"),
        P(None, "lat", "lon"),
        P(None, ("lat", "lon")),
    )
    return jax.shard_map(local, mesh=mesh, in_specs=in_specs, out_specs=out_specs, check_vma=False)
```
